128 devices in a mesh: gx: 16 (over z, x), gy: 8 (over y, core).
Axes of the slice: x: 4, y: 4, z: 4, core: 2. Of those that a mesh axis runs over, the one named last changes fastest.
Arguments:
- parent_field: float32 [8, 2048, 4096], P(None, 'gx', 'gy'), may hold values from -6 to 6
- parent_sppt: bfloat16 [2048, 4096], P('gx', 'gy'), may hold values from -0.796875 to 0.796875
- child_storm: float32 [8, 2048, 3072], P(None, 'gx', 'gy'), may hold values from -6 to 6
- child_sppt: bfloat16 [2048, 3072], P('gx', 'gy'), may hold values from -0.796875 to 0.796875
- wind: float32 [2, 8], replicated, may hold values from -0.3 to 0.3
- strip_dest: int32 [16384, 1], replicated, may hold values from 0 to 127; in each aligned block of 128 rows (0 to 127, 128 to 255, ...) at most 2 rows name the same one
- strip_row: int32 [16384], replicated, may hold values from 0 to 511
- strip_target: int32 [16384], replicated, may hold values from 0 to 127
- storm_shift: int32 [2, 4], replicated, may hold values from 0 to 15, as said below
Outputs:
- new_parent: float32 [8, 2048, 4096], P(None, 'gx', 'gy')
- child: float32 [8, 2048, 3072], P(None, 'gx', 'gy')
The draws below stay inside these ranges and needn't reach their ends.
Inputs may be any that keep to these rules, and one draw needn't show every extreme that they name: `strip_dest`: among the 128 strips of one parent device no owner appears more than 2 times. `storm_shift`: row 0 lies in 0 to 16 - 1 and holds 16 - 1 at least once; row 1 lies in 0 to 8 - 1 and holds 8 - 1 at least once.
All inputs are finite; a program needn't handle non-finite values.
Results may differ from the reference program's by a relative error of at most 0.0003.
Values sent between devices are 32-bit elements; how exact they have to be, the bound alone decides.
No kernel may reach another device: no remote copies, remote signals or barrier semaphores. Data moves between devices by JAX's collectives and lax.ppermute only.
A program may use at most 64 MiB of HBM per device.

```python
import math
import jax
import jax.numpy as jnp
import numpy as np
from jax import lax

LEV = 8
SUBSTEPS = 3
STRIP = 128
CAP = 2
NPIECE = 4
PBX = 128
PBY = 512
CROWS = 128
SLOTS = 128
PX = 32
CY = 384
NRB = 512
NPX = 2048
NPY = 4096
NCX = 2048
NCY = 3072
N_GX = 16
N_GY = 8
DEVICES = 128


def draw_storm_shift(key, part):
    keys = jax.random.split(key, 4)
    count_x = NCX // CROWS
    count_y = NCY // CY
    places = jnp.arange(NPIECE)
    shift_x = jax.random.randint(keys[0], (NPIECE,), 0, count_x)
    where_x = jax.random.randint(keys[1], (), 0, NPIECE)
    shift_x = jnp.where(places == where_x, count_x - 1, shift_x)
    shift_y = jax.random.randint(keys[2], (NPIECE,), 0, count_y)
    where_y = jax.random.randint(keys[3], (), 0, NPIECE)
    shift_y = jnp.where(places == where_y, count_y - 1, shift_y)
    return jnp.stack([shift_x, shift_y]).astype(jnp.int32)


def touch_ends(values, own_key, smallest, top_value):
    spot = [jax.random.randint(jax.random.fold_in(own_key, axis), (), 0, length) for axis, length in enumerate(values.shape)]
    main_axis = values.shape.index(max(values.shape))
    neighbour = spot[:main_axis] + [(spot[main_axis] + 1) % values.shape[main_axis]] + spot[main_axis + 1:]
    return values.at[tuple(spot)].set(smallest).at[tuple(neighbour)].set(top_value)


def levels(rng, shape, pieces, least, high):
    level, own = 1.0, jax.random.fold_in(rng, 6)
    for dim, shards_of in pieces:
        steps = jnp.exp(jax.random.uniform(jax.random.fold_in(own, dim), (shards_of,), jnp.float32, least / len(pieces), high / len(pieces)))
        level = level * jnp.repeat(steps, shape[dim] // shards_of).reshape([-1 if axis == dim else 1 for axis in range(len(shape))])
    return level


def deal_out(rng, own, number, rows, count, top, bound, lean):
    sequence = jax.random.permutation(rng, count)
    crowded, ordinary = shares(count, rows * top, bound, lean, True), shares(count, rows * top, bound, lean, False)
    places = jnp.arange(count)

    def named(lengths, turn):
        used = int((lengths > 0).sum())
        fixed = max(1, used // 4)
        passed = fixed + (places - fixed + turn * (used - fixed)) % max(1, count - fixed)
        return jnp.zeros((count,), jnp.int32).at[sequence[jnp.where(places < fixed, places, passed)]].set(jnp.asarray(lengths, jnp.int32))

    lengths = jnp.where(number % 4 == 0, named(crowded, number // 4), named(ordinary, number - number // 4 - 1))
    mixed = jax.random.permutation(jax.random.fold_in(own, 3), count)
    donor, receiver = mixed[0:count // 2 * 2:2], mixed[1:count // 2 * 2:2]
    slack = jnp.minimum(lengths[donor] - 1, bound - lengths[receiver]) // 2
    slack = jnp.where((donor == sequence[0]) | (receiver == sequence[0]) | (lengths[receiver] == 0), 0, jnp.maximum(slack, 0))
    passed = jax.random.randint(jax.random.fold_in(own, 4), (count // 2,), 0, 1 << 20) % (slack + 1)
    lengths = lengths.at[donor].add(-passed).at[receiver].add(passed)
    members = jnp.searchsorted(jnp.cumsum(lengths), jnp.arange(rows * top), side="right").astype(jnp.int32)
    grid = members.reshape(top, rows).T
    grid = grid[jax.random.permutation(jax.random.fold_in(own, 1), rows)]
    turn = jax.random.randint(jax.random.fold_in(own, 2), (rows, 1), 0, top)
    return jnp.take_along_axis(grid, (jnp.arange(top)[None, :] + turn) % top, axis=1)


def shares(amount, total, reach, slope, full):
    loads = [(1 << 20) // math.isqrt(standing ** slope) + 1 for standing in range(1, amount + 1)]
    largest = reach if full else min(reach, max(-(-total // amount), total * loads[0] // sum(loads)))
    least = 1 if total - largest >= amount - 1 else 0
    holding, spare = [largest] + [least] * (amount - 1), total - largest - least * (amount - 1)
    while spare > 0:
        movable = [i for i in range(1, amount) if holding[i] < largest] or [i for i in range(1, amount) if holding[i] < reach]
        mass, left = sum([loads[i] for i in movable]), spare
        for i in movable:
            addition = min(reach - holding[i], max(1, left * loads[i] // mass), spare)
            holding[i] = holding[i] + addition
            spare = spare - addition
    return np.array(holding)


def centred(own_key, dims, scale, most, cuts=(), kind=jnp.bfloat16):
    level = levels(own_key, dims, cuts, -0.22, 0.18) if cuts else 1.0
    result = jax.random.normal(own_key, dims, jnp.float32) * scale * level
    return jnp.minimum(jnp.maximum(result, -most), most).astype(kind)


def setup_inputs(seed: int = 0) -> dict:
    arg_keys = jax.random.split(jax.random.key(seed), 10)
    parent_field = centred(arg_keys[0], (LEV, NPX, NPY), 1.0, 6.0, ((1, 16), (2, 8)), jnp.float32)
    parent_sppt = jnp.clip(jax.random.uniform(arg_keys[1], (NPX, NPY), jnp.float32, -0.796875, 0.796875) * levels(arg_keys[1], (NPX, NPY), ((0, 16), (1, 8)), -0.4, 0.0), -0.796875, 0.796875).astype(jnp.bfloat16)
    child_storm = centred(arg_keys[2], (LEV, NCX, NCY), 1.0, 6.0, ((1, 16), (2, 8)), jnp.float32)
    child_sppt = jnp.clip(jax.random.uniform(arg_keys[3], (NCX, NCY), jnp.float32, -0.796875, 0.796875) * levels(arg_keys[3], (NCX, NCY), ((0, 16), (1, 8)), -0.4, 0.0), -0.796875, 0.796875).astype(jnp.bfloat16)
    wind = jnp.clip(jax.random.uniform(arg_keys[4], (2, LEV), jnp.float32, -0.3, 0.3), -0.3, 0.3)
    strip_dest_keys = jax.random.split(jax.random.fold_in(arg_keys[5], 1), (DEVICES * SLOTS) // SLOTS)
    strip_dest_turns = jax.random.permutation(jax.random.fold_in(arg_keys[5], 3), (DEVICES * SLOTS) // SLOTS)
    strip_dest = jax.vmap(lambda own, number: deal_out(jax.random.fold_in(arg_keys[5], 2), own, number, SLOTS, DEVICES, 1, CAP, 2))(strip_dest_keys, strip_dest_turns).reshape((DEVICES * SLOTS, 1))
    strip_row = touch_ends(jax.random.randint(arg_keys[6], (DEVICES * SLOTS,), 0, NRB), jax.random.fold_in(arg_keys[6], 1), 0, NRB - 1).astype(jnp.int32)
    strip_target = touch_ends(jax.random.randint(arg_keys[7], (DEVICES * SLOTS,), 0, CROWS), jax.random.fold_in(arg_keys[7], 1), 0, CROWS - 1).astype(jnp.int32)
    storm_shift = draw_storm_shift(jax.random.fold_in(arg_keys[9], 71), 0)
    return dict(parent_field=parent_field, parent_sppt=parent_sppt, child_storm=child_storm, child_sppt=child_sppt, wind=wind, strip_dest=strip_dest, strip_row=strip_row, strip_target=strip_target, storm_shift=storm_shift)


KAPPA = 0.1
VERTICAL = 0.1
NUDGE = 0.5


def refine_table(strip):
    coarse = jnp.arange(strip).astype(jnp.float32)
    finer = jnp.arange(3 * strip).astype(jnp.float32)
    position = jnp.clip((finer + 0.5) / 3.0 - 0.5, 0.0, strip - 1.0)
    return jnp.maximum(0.0, 1.0 - jnp.abs(position[None, :] - coarse[:, None]))


def tendency(padded, wind_x, wind_y):
    centre = padded[..., 1:-1, 1:-1]
    north = padded[..., 2:, 1:-1]
    south = padded[..., :-2, 1:-1]
    east = padded[..., 1:-1, 2:]
    west = padded[..., 1:-1, :-2]
    laplace = north + south + east + west - 4.0 * centre
    return KAPPA * laplace - wind_x * (0.5 * (north - south)) - wind_y * (0.5 * (east - west))


def vertical(field):
    upper = jnp.concatenate([field[1:], field[-1:]], axis=0)
    lower = jnp.concatenate([field[:1], field[:-1]], axis=0)
    return upper + lower - 2.0 * field


def reference(parent_field, parent_sppt, child_storm, child_sppt, wind, strip_dest, strip_row, strip_target, storm_shift):
    devices = N_GX * N_GY
    wind_x = wind[0][:, None, None]
    wind_y = wind[1][:, None, None]
    padded = jnp.pad(parent_field, ((0, 0), (1, 1), (1, 1)))
    new_parent = parent_field + (1.0 + parent_sppt.astype(jnp.float32)) * (
        tendency(padded, wind_x, wind_y) + VERTICAL * vertical(parent_field))

    def device_rows(field):
        blocks = field.reshape(LEV, N_GX, PBX, N_GY, PBY).transpose(1, 3, 0, 2, 4)
        return blocks.reshape(devices, LEV, NRB, STRIP)

    source = jnp.repeat(jnp.arange(devices, dtype=jnp.int32), SLOTS)
    old_values = device_rows(parent_field)[source, :, strip_row]
    new_values = device_rows(new_parent)[source, :, strip_row]
    total = devices * SLOTS
    data = jnp.stack([old_values, new_values], axis=1).reshape(total, 2 * LEV * STRIP)
    segment = (strip_dest[:, 0] * CROWS + strip_target).astype(jnp.int32)
    coarse = jax.ops.segment_sum(data, segment, num_segments=devices * CROWS)
    counts = jax.ops.segment_sum(jnp.ones((total,), jnp.float32), segment, num_segments=devices * CROWS)
    counts_grid = counts.reshape(N_GX, N_GY, CROWS).transpose(0, 2, 1).reshape(NCX, N_GY)
    counts_grid = jnp.repeat(counts_grid, CY, axis=1)
    coarse_levels = coarse.reshape(N_GX, N_GY, CROWS, 2, LEV, STRIP).transpose(4, 3, 0, 2, 1, 5)
    coarse_levels = coarse_levels.reshape(LEV, 2, NCX, N_GY, STRIP)

    blocks = child_storm.reshape(LEV, N_GX, NPIECE, PX, N_GY, CY)
    bands = []
    for piece in range(NPIECE):
        band = blocks[:, :, piece]
        band = jnp.roll(band, storm_shift[0, piece], axis=1)
        band = jnp.roll(band, storm_shift[1, piece], axis=3)
        bands.append(band)
    child_start = jnp.stack(bands, axis=2).reshape(LEV, NCX, NCY)

    table = refine_table(STRIP)
    factor = 1.0 + child_sppt.astype(jnp.float32)
    divisor = 1.0 + NUDGE * counts_grid

    def level_step(items):
        field, coarse_level, wind_pair = items
        boundary = jnp.einsum('axnd,de->axne', coarse_level, table,
                              precision=lax.Precision.HIGHEST).reshape(2, NCX, NCY)
        for substep in range(SUBSTEPS):
            padded_level = jnp.pad(field, 1)
            weight = (substep + 1) / 3.0
            target_value = boundary[0] + weight * (boundary[1] - boundary[0])
            field = (field + factor * tendency(padded_level, wind_pair[0], wind_pair[1])
                     + NUDGE * target_value) / divisor
        return field

    child = lax.map(level_step, (child_start, coarse_levels, wind.T))
    return new_parent, child
```

```python
import jax
import jax.numpy as jnp
from jax import lax
from jax.sharding import PartitionSpec as P

SUBSTEPS = 3
STRIP = 128
CAP = 2


KAPPA = 0.1
VERTICAL = 0.1
NUDGE = 0.5


def padded_2(block, sides, width):
    for axis, dim in sides:
        count = lax.axis_size(axis)
        forward = [(i, i + 1) for i in range(count - 1)]
        backward = [(target, source) for source, target in forward]
        low = lax.ppermute(
            lax.slice_in_dim(block, block.shape[dim] - width, None, axis=dim), axis, forward
        )
        high = lax.ppermute(lax.slice_in_dim(block, 0, width, axis=dim), axis, backward)
        block = jnp.concatenate([low, block, high], axis=dim)
    return block


def from_behind(value, axis, steps):
    count = lax.axis_size(axis)
    pairs = [(source, (source + steps) % count) for source in range(count)]
    return lax.ppermute(value, axis, pairs)


def shift_by(axis, steps):
    def move(value):
        if steps == 0:
            return value
        return from_behind(value, axis, steps)

    return move


def shift_bands(child, storm_shift, band_rows):
    npiece = storm_shift.shape[1]
    branches = {
        axis: [shift_by(axis, s) for s in range(lax.axis_size(axis))] for axis in ("gx", "gy")
    }

    def one_band(piece, moved):
        start = piece * band_rows
        band = lax.dynamic_slice_in_dim(child, start, band_rows, axis=1)
        for row, axis in ((1, "gy"), (0, "gx")):
            band = lax.switch(storm_shift[row, piece], branches[axis], band)
        return lax.dynamic_update_slice_in_dim(moved, band, start, axis=1)

    return lax.fori_loop(0, npiece, one_band, jnp.zeros_like(child))


def refine_table(strip):
    coarse = jnp.arange(strip).astype(jnp.float32)
    finer = jnp.arange(3 * strip).astype(jnp.float32)
    position = jnp.clip((finer + 0.5) / 3.0 - 0.5, 0.0, strip - 1.0)
    return jnp.maximum(0.0, 1.0 - jnp.abs(position[None, :] - coarse[:, None]))


def tendency(padded, wind_x, wind_y):
    centre = padded[..., 1:-1, 1:-1]
    north = padded[..., 2:, 1:-1]
    south = padded[..., :-2, 1:-1]
    east = padded[..., 1:-1, 2:]
    west = padded[..., 1:-1, :-2]
    laplace = north + south + east + west - 4.0 * centre
    return KAPPA * laplace - wind_x * (0.5 * (north - south)) - wind_y * (0.5 * (east - west))


def vertical(field):
    upper = jnp.concatenate([field[1:], field[-1:]], axis=0)
    lower = jnp.concatenate([field[:1], field[:-1]], axis=0)
    return upper + lower - 2.0 * field


def shards(
    parent_field,
    parent_sppt,
    child_storm,
    child_sppt,
    wind,
    strip_dest,
    strip_row,
    strip_target,
    storm_shift,
):
    devices = lax.axis_size(("gx", "gy"))
    my_index = lax.axis_index(("gx", "gy"))
    wind_x = wind[0][:, None, None]
    wind_y = wind[1][:, None, None]
    padded = padded_2(parent_field, (("gx", 1), ("gy", 2)), 1)
    new_parent = parent_field + (1.0 + parent_sppt.astype(jnp.float32)) * (
        tendency(padded, wind_x, wind_y) + VERTICAL * vertical(parent_field)
    )
    levels, crows, widths = child_storm.shape
    npiece = storm_shift.shape[1]
    band_rows = crows // npiece
    col_count = lax.axis_size("gy")
    child = shift_bands(child_storm, storm_shift, band_rows)
    dest_table = strip_dest.reshape(devices, -1)
    row_table = strip_row.reshape(devices, -1)
    target_table = strip_target.reshape(devices, -1)
    slots = dest_table.shape[1]
    my_dest = lax.dynamic_index_in_dim(dest_table, my_index, 0, keepdims=False)
    my_rows = lax.dynamic_index_in_dim(row_table, my_index, 0, keepdims=False)
    same_owner = my_dest[:, None] == my_dest[None, :]
    earlier = jnp.arange(slots)[None, :] < jnp.arange(slots)[:, None]
    rank = jnp.sum((same_owner & earlier).astype(jnp.int32), axis=1)
    slot_index = my_dest * CAP + rank
    send_select = (jnp.arange(devices * CAP)[:, None] == slot_index[None, :]).astype(jnp.float32)
    both_states = jnp.stack([parent_field, new_parent]).reshape(2, levels, -1, STRIP)
    picked = jnp.take(both_states, my_rows, axis=2)
    strip_values = jnp.moveaxis(picked, 2, 0).reshape(slots, -1)
    outgoing_strips = jnp.dot(
        send_select,
        strip_values,
        precision=lax.Precision.HIGHEST,
        preferred_element_type=jnp.float32,
    )
    incoming = lax.all_to_all(
        outgoing_strips, ("gx", "gy"), split_axis=0, concat_axis=0, tiled=True
    )
    mine = dest_table == my_index
    rank_all = jnp.cumsum(mine.astype(jnp.int32), axis=1) - 1
    slot_ids = jnp.arange(CAP)
    hits = mine[:, None, :] & (rank_all[:, None, :] == slot_ids[None, :, None])
    chosen = jnp.sum(jnp.where(hits, target_table[:, None, :], 0), axis=2)
    target_rows = jnp.where(jnp.any(hits, axis=2), chosen, -1).reshape(-1)
    row_select = (jnp.arange(crows)[:, None] == target_rows[None, :]).astype(jnp.float32)
    coarse = jnp.dot(
        row_select, incoming, precision=lax.Precision.HIGHEST, preferred_element_type=jnp.float32
    )
    counts = jnp.sum(row_select, axis=1)
    boundary = jnp.einsum(
        "tald,de->alte",
        coarse.reshape(crows, 2, levels, STRIP),
        refine_table(STRIP),
        precision=lax.Precision.HIGHEST,
    )
    divisor = 1.0 + NUDGE * counts[None, :, None]
    factor = 1.0 + child_sppt.astype(jnp.float32)
    for substep in range(SUBSTEPS):
        padded_child = padded_2(child, (("gx", 1), ("gy", 2)), 1)
        weight = (substep + 1) / 3.0
        target_value = boundary[0] + weight * (boundary[1] - boundary[0])
        child = (
            child + factor * tendency(padded_child, wind_x, wind_y) + NUDGE * target_value
        ) / divisor
    return (new_parent, child)


def solution(mesh):
    placed = (
        P(None, "gx", "gy"),
        P("gx", "gy"),
        P(None, "gx", "gy"),
        P("gx", "gy"),
        P(),
        P(),
        P(),
        P(),
        P(),
    )
    return jax.shard_map(
        shards,
        mesh=mesh,
        in_specs=placed,
        out_specs=(P(None, "gx", "gy"), P(None, "gx", "gy")),
        check_vma=False,
    )
```

```python
import jax
import jax.numpy as jnp
from jax import lax
from jax.sharding import PartitionSpec as P

SUBSTEPS = 3
STRIP = 128
CAP = 2


KAPPA = 0.1
VERTICAL = 0.1
NUDGE = 0.5


def padded_2(block, sides, width):
    for axis, dim in sides:
        count = lax.axis_size(axis)
        forward = [(i, i + 1) for i in range(count - 1)]
        backward = [(target, source) for source, target in forward]
        low = lax.ppermute(
            lax.slice_in_dim(block, block.shape[dim] - width, None, axis=dim), axis, forward
        )
        high = lax.ppermute(lax.slice_in_dim(block, 0, width, axis=dim), axis, backward)
        block = jnp.concatenate([low, block, high], axis=dim)
    return block


def from_behind(value, axis, steps):
    count = lax.axis_size(axis)
    pairs = [(source, (source + steps) % count) for source in range(count)]
    return lax.ppermute(value, axis, pairs)


def shift_by(nx, ny, sx, sy):
    def move(value):
        if sx == 0 and sy == 0:
            return value
        pairs = [
            (jx * ny + jy, (jx + sx) % nx * ny + (jy + sy) % ny)
            for jx in range(nx)
            for jy in range(ny)
        ]
        return lax.ppermute(value, ("gx", "gy"), pairs)

    return move


def shift_bands(child, storm_shift, band_rows):
    npiece = storm_shift.shape[1]
    nx, ny = lax.axis_size("gx"), lax.axis_size("gy")
    branches = [shift_by(nx, ny, sx, sy) for sx in range(nx) for sy in range(ny)]

    def one_band(piece, moved):
        start = piece * band_rows
        band = lax.dynamic_slice_in_dim(child, start, band_rows, axis=1)
        which = storm_shift[0, piece] * ny + storm_shift[1, piece]
        band = lax.switch(which, branches, band)
        return lax.dynamic_update_slice_in_dim(moved, band, start, axis=1)

    return lax.fori_loop(0, npiece, one_band, jnp.zeros_like(child))


def refine_table(strip):
    coarse = jnp.arange(strip).astype(jnp.float32)
    finer = jnp.arange(3 * strip).astype(jnp.float32)
    position = jnp.clip((finer + 0.5) / 3.0 - 0.5, 0.0, strip - 1.0)
    return jnp.maximum(0.0, 1.0 - jnp.abs(position[None, :] - coarse[:, None]))


def tendency(padded, wind_x, wind_y):
    centre = padded[..., 1:-1, 1:-1]
    north = padded[..., 2:, 1:-1]
    south = padded[..., :-2, 1:-1]
    east = padded[..., 1:-1, 2:]
    west = padded[..., 1:-1, :-2]
    laplace = north + south + east + west - 4.0 * centre
    return KAPPA * laplace - wind_x * (0.5 * (north - south)) - wind_y * (0.5 * (east - west))


def vertical(field):
    upper = jnp.concatenate([field[1:], field[-1:]], axis=0)
    lower = jnp.concatenate([field[:1], field[:-1]], axis=0)
    return upper + lower - 2.0 * field


def shards(
    parent_field,
    parent_sppt,
    child_storm,
    child_sppt,
    wind,
    strip_dest,
    strip_row,
    strip_target,
    storm_shift,
):
    devices = lax.axis_size(("gx", "gy"))
    my_index = lax.axis_index(("gx", "gy"))
    wind_x = wind[0][:, None, None]
    wind_y = wind[1][:, None, None]
    padded = padded_2(parent_field, (("gx", 1), ("gy", 2)), 1)
    new_parent = parent_field + (1.0 + parent_sppt.astype(jnp.float32)) * (
        tendency(padded, wind_x, wind_y) + VERTICAL * vertical(parent_field)
    )
    levels, crows, widths = child_storm.shape
    npiece = storm_shift.shape[1]
    band_rows = crows // npiece
    col_count = lax.axis_size("gy")
    child = shift_bands(child_storm, storm_shift, band_rows)
    dest_table = strip_dest.reshape(devices, -1)
    row_table = strip_row.reshape(devices, -1)
    target_table = strip_target.reshape(devices, -1)
    slots = dest_table.shape[1]
    my_dest = lax.dynamic_index_in_dim(dest_table, my_index, 0, keepdims=False)
    my_rows = lax.dynamic_index_in_dim(row_table, my_index, 0, keepdims=False)
    same_owner = my_dest[:, None] == my_dest[None, :]
    earlier = jnp.arange(slots)[None, :] < jnp.arange(slots)[:, None]
    rank = jnp.sum((same_owner & earlier).astype(jnp.int32), axis=1)
    slot_index = my_dest * CAP + rank
    send_select = (jnp.arange(devices * CAP)[:, None] == slot_index[None, :]).astype(jnp.float32)
    both_states = jnp.stack([parent_field, new_parent]).reshape(2, levels, -1, STRIP)
    picked = jnp.take(both_states, my_rows, axis=2)
    strip_values = jnp.moveaxis(picked, 2, 0).reshape(slots, -1)
    outgoing_strips = jnp.dot(
        send_select,
        strip_values,
        precision=lax.Precision.HIGHEST,
        preferred_element_type=jnp.float32,
    )
    incoming = lax.all_to_all(
        outgoing_strips, ("gx", "gy"), split_axis=0, concat_axis=0, tiled=True
    )
    mine = dest_table == my_index
    rank_all = jnp.cumsum(mine.astype(jnp.int32), axis=1) - 1
    slot_ids = jnp.arange(CAP)
    hits = mine[:, None, :] & (rank_all[:, None, :] == slot_ids[None, :, None])
    chosen = jnp.sum(jnp.where(hits, target_table[:, None, :], 0), axis=2)
    target_rows = jnp.where(jnp.any(hits, axis=2), chosen, -1).reshape(-1)
    row_select = (jnp.arange(crows)[:, None] == target_rows[None, :]).astype(jnp.float32)
    coarse = jnp.dot(
        row_select, incoming, precision=lax.Precision.HIGHEST, preferred_element_type=jnp.float32
    )
    counts = jnp.sum(row_select, axis=1)
    boundary = jnp.einsum(
        "tald,de->alte",
        coarse.reshape(crows, 2, levels, STRIP),
        refine_table(STRIP),
        precision=lax.Precision.HIGHEST,
    )
    divisor = 1.0 + NUDGE * counts[None, :, None]
    factor = 1.0 + child_sppt.astype(jnp.float32)
    for substep in range(SUBSTEPS):
        padded_child = padded_2(child, (("gx", 1), ("gy", 2)), 1)
        weight = (substep + 1) / 3.0
        target_value = boundary[0] + weight * (boundary[1] - boundary[0])
        child = (
            child + factor * tendency(padded_child, wind_x, wind_y) + NUDGE * target_value
        ) / divisor
    return (new_parent, child)


def solution(mesh):
    placed = (
        P(None, "gx", "gy"),
        P("gx", "gy"),
        P(None, "gx", "gy"),
        P("gx", "gy"),
        P(),
        P(),
        P(),
        P(),
        P(),
    )
    return jax.shard_map(
        shards,
        mesh=mesh,
        in_specs=placed,
        out_specs=(P(None, "gx", "gy"), P(None, "gx", "gy")),
        check_vma=False,
    )
```

```python
import jax
import jax.numpy as jnp
from jax import lax
from jax.sharding import PartitionSpec as P

SUBSTEPS = 3
STRIP = 128
CAP = 2


KAPPA = 0.1
VERTICAL = 0.1
NUDGE = 0.5


def padded_2(block, sides, width):
    for axis, dim in sides:
        count = lax.axis_size(axis)
        forward = [(i, i + 1) for i in range(count - 1)]
        backward = [(target, source) for source, target in forward]
        low = lax.ppermute(
            lax.slice_in_dim(block, block.shape[dim] - width, None, axis=dim), axis, forward
        )
        high = lax.ppermute(lax.slice_in_dim(block, 0, width, axis=dim), axis, backward)
        block = jnp.concatenate([low, block, high], axis=dim)
    return block


def from_behind(value, axis, steps):
    count = lax.axis_size(axis)
    pairs = [(source, (source + steps) % count) for source in range(count)]
    return lax.ppermute(value, axis, pairs)


def storm_pieces(child, npiece, devices):
    levels, crows, widths = child.shape
    band_rows = crows // npiece
    per_level = devices // levels
    pieces = child.reshape(levels, npiece, per_level, band_rows // per_level, widths)
    return jnp.transpose(pieces, (0, 2, 1, 3, 4)).reshape(devices, npiece, -1)


def storm_unpieces(pieces, levels, crows, widths):
    devices, npiece = pieces.shape[:2]
    per_level = devices // levels
    child = pieces.reshape(levels, per_level, npiece, crows // npiece // per_level, widths)
    return jnp.transpose(child, (0, 2, 1, 3, 4)).reshape(levels, crows, widths)


def storm_sources(storm_shift, nx, ny):
    dest = jnp.arange(nx * ny)
    src_x = (dest[:, None] // ny - storm_shift[0][None, :]) % nx
    src_y = (dest[:, None] % ny - storm_shift[1][None, :]) % ny
    return src_x * ny + src_y


def refine_table(strip):
    coarse = jnp.arange(strip).astype(jnp.float32)
    finer = jnp.arange(3 * strip).astype(jnp.float32)
    position = jnp.clip((finer + 0.5) / 3.0 - 0.5, 0.0, strip - 1.0)
    return jnp.maximum(0.0, 1.0 - jnp.abs(position[None, :] - coarse[:, None]))


def tendency(padded, wind_x, wind_y):
    centre = padded[..., 1:-1, 1:-1]
    north = padded[..., 2:, 1:-1]
    south = padded[..., :-2, 1:-1]
    east = padded[..., 1:-1, 2:]
    west = padded[..., 1:-1, :-2]
    laplace = north + south + east + west - 4.0 * centre
    return KAPPA * laplace - wind_x * (0.5 * (north - south)) - wind_y * (0.5 * (east - west))


def vertical(field):
    upper = jnp.concatenate([field[1:], field[-1:]], axis=0)
    lower = jnp.concatenate([field[:1], field[:-1]], axis=0)
    return upper + lower - 2.0 * field


def shards(
    parent_field,
    parent_sppt,
    child_storm,
    child_sppt,
    wind,
    strip_dest,
    strip_row,
    strip_target,
    storm_shift,
):
    devices = lax.axis_size(("gx", "gy"))
    my_index = lax.axis_index(("gx", "gy"))
    wind_x = wind[0][:, None, None]
    wind_y = wind[1][:, None, None]
    padded = padded_2(parent_field, (("gx", 1), ("gy", 2)), 1)
    new_parent = parent_field + (1.0 + parent_sppt.astype(jnp.float32)) * (
        tendency(padded, wind_x, wind_y) + VERTICAL * vertical(parent_field)
    )
    levels, crows, widths = child_storm.shape
    npiece = storm_shift.shape[1]
    band_rows = crows // npiece
    col_count = lax.axis_size("gy")
    nx, ny = lax.axis_size("gx"), lax.axis_size("gy")
    gathered = lax.all_to_all(
        storm_pieces(child_storm, npiece, devices), ("gx", "gy"), 0, 0, tiled=True
    )
    sources = storm_sources(storm_shift, nx, ny)
    storm_out = jnp.take_along_axis(gathered, sources[:, :, None], axis=0)
    dest_table = strip_dest.reshape(devices, -1)
    row_table = strip_row.reshape(devices, -1)
    target_table = strip_target.reshape(devices, -1)
    slots = dest_table.shape[1]
    my_dest = lax.dynamic_index_in_dim(dest_table, my_index, 0, keepdims=False)
    my_rows = lax.dynamic_index_in_dim(row_table, my_index, 0, keepdims=False)
    same_owner = my_dest[:, None] == my_dest[None, :]
    earlier = jnp.arange(slots)[None, :] < jnp.arange(slots)[:, None]
    rank = jnp.sum((same_owner & earlier).astype(jnp.int32), axis=1)
    slot_index = my_dest * CAP + rank
    send_select = (jnp.arange(devices * CAP)[:, None] == slot_index[None, :]).astype(jnp.float32)
    both_states = jnp.stack([parent_field, new_parent]).reshape(2, levels, -1, STRIP)
    picked = jnp.take(both_states, my_rows, axis=2)
    strip_values = jnp.moveaxis(picked, 2, 0).reshape(slots, -1)
    outgoing_strips = jnp.dot(
        send_select,
        strip_values,
        precision=lax.Precision.HIGHEST,
        preferred_element_type=jnp.float32,
    )
    strip_width = outgoing_strips.shape[1]
    outgoing = jnp.concatenate(
        [outgoing_strips.reshape(devices, -1), storm_out.reshape(devices, -1)], axis=1
    )
    arrived = lax.all_to_all(outgoing, ("gx", "gy"), split_axis=0, concat_axis=0, tiled=True)
    strip_part = CAP * strip_width
    incoming = arrived[:, :strip_part].reshape(devices * CAP, strip_width)
    child = storm_unpieces(
        arrived[:, strip_part:].reshape(devices, npiece, -1), levels, crows, widths
    )
    mine = dest_table == my_index
    rank_all = jnp.cumsum(mine.astype(jnp.int32), axis=1) - 1
    slot_ids = jnp.arange(CAP)
    hits = mine[:, None, :] & (rank_all[:, None, :] == slot_ids[None, :, None])
    chosen = jnp.sum(jnp.where(hits, target_table[:, None, :], 0), axis=2)
    target_rows = jnp.where(jnp.any(hits, axis=2), chosen, -1).reshape(-1)
    row_select = (jnp.arange(crows)[:, None] == target_rows[None, :]).astype(jnp.float32)
    coarse = jnp.dot(
        row_select, incoming, precision=lax.Precision.HIGHEST, preferred_element_type=jnp.float32
    )
    counts = jnp.sum(row_select, axis=1)
    boundary = jnp.einsum(
        "tald,de->alte",
        coarse.reshape(crows, 2, levels, STRIP),
        refine_table(STRIP),
        precision=lax.Precision.HIGHEST,
    )
    divisor = 1.0 + NUDGE * counts[None, :, None]
    factor = 1.0 + child_sppt.astype(jnp.float32)
    for substep in range(SUBSTEPS):
        padded_child = padded_2(child, (("gx", 1), ("gy", 2)), 1)
        weight = (substep + 1) / 3.0
        target_value = boundary[0] + weight * (boundary[1] - boundary[0])
        child = (
            child + factor * tendency(padded_child, wind_x, wind_y) + NUDGE * target_value
        ) / divisor
    return (new_parent, child)


def solution(mesh):
    placed = (
        P(None, "gx", "gy"),
        P("gx", "gy"),
        P(None, "gx", "gy"),
        P("gx", "gy"),
        P(),
        P(),
        P(),
        P(),
        P(),
    )
    return jax.shard_map(
        shards,
        mesh=mesh,
        in_specs=placed,
        out_specs=(P(None, "gx", "gy"), P(None, "gx", "gy")),
        check_vma=False,
    )
```

```python
import jax
import jax.numpy as jnp
from jax import lax
from jax.sharding import PartitionSpec as P

SUBSTEPS = 3
STRIP = 128
CAP = 2


KAPPA = 0.1
VERTICAL = 0.1
NUDGE = 0.5


def edge_halos(block):
    def swap(edge, axis, forward):
        count = lax.axis_size(axis)
        pairs = [(i, i + 1) for i in range(count - 1)]
        if not forward:
            pairs = [(target, source) for source, target in pairs]
        return lax.ppermute(edge, axis, pairs)

    before_x = swap(block[:, -1, :], "gx", True)
    after_x = swap(block[:, 0, :], "gx", False)
    before_y = swap(block[:, :, -1], "gy", True)
    after_y = swap(block[:, :, 0], "gy", False)
    return before_x, after_x, before_y, after_y


def halo_tendency(block, wind_x, wind_y):
    before_x, after_x, before_y, after_y = edge_halos(block)
    north = jnp.concatenate([block[:, 1:, :], after_x[:, None, :]], axis=1)
    south = jnp.concatenate([before_x[:, None, :], block[:, :-1, :]], axis=1)
    east = jnp.concatenate([block[:, :, 1:], after_y[:, :, None]], axis=2)
    west = jnp.concatenate([before_y[:, :, None], block[:, :, :-1]], axis=2)
    laplace = north + south + east + west - 4.0 * block
    return KAPPA * laplace - wind_x * (0.5 * (north - south)) - wind_y * (0.5 * (east - west))


def from_behind(value, axis, steps):
    count = lax.axis_size(axis)
    pairs = [(source, (source + steps) % count) for source in range(count)]
    return lax.ppermute(value, axis, pairs)


def storm_pieces(child, npiece, devices):
    levels, crows, widths = child.shape
    band_rows = crows // npiece
    per_level = devices // levels
    pieces = child.reshape(levels, npiece, per_level, band_rows // per_level, widths)
    return jnp.transpose(pieces, (0, 2, 1, 3, 4)).reshape(devices, npiece, -1)


def storm_unpieces(pieces, levels, crows, widths):
    devices, npiece = pieces.shape[:2]
    per_level = devices // levels
    child = pieces.reshape(levels, per_level, npiece, crows // npiece // per_level, widths)
    return jnp.transpose(child, (0, 2, 1, 3, 4)).reshape(levels, crows, widths)


def storm_sources(storm_shift, nx, ny):
    dest = jnp.arange(nx * ny)
    src_x = (dest[:, None] // ny - storm_shift[0][None, :]) % nx
    src_y = (dest[:, None] % ny - storm_shift[1][None, :]) % ny
    return src_x * ny + src_y


def refine_table(strip):
    coarse = jnp.arange(strip).astype(jnp.float32)
    finer = jnp.arange(3 * strip).astype(jnp.float32)
    position = jnp.clip((finer + 0.5) / 3.0 - 0.5, 0.0, strip - 1.0)
    return jnp.maximum(0.0, 1.0 - jnp.abs(position[None, :] - coarse[:, None]))


def vertical(field):
    upper = jnp.concatenate([field[1:], field[-1:]], axis=0)
    lower = jnp.concatenate([field[:1], field[:-1]], axis=0)
    return upper + lower - 2.0 * field


def shards(
    parent_field,
    parent_sppt,
    child_storm,
    child_sppt,
    wind,
    strip_dest,
    strip_row,
    strip_target,
    storm_shift,
):
    devices = lax.axis_size(("gx", "gy"))
    my_index = lax.axis_index(("gx", "gy"))
    wind_x = wind[0][:, None, None]
    wind_y = wind[1][:, None, None]
    new_parent = parent_field + (1.0 + parent_sppt.astype(jnp.float32)) * (
        halo_tendency(parent_field, wind_x, wind_y) + VERTICAL * vertical(parent_field)
    )
    levels, crows, widths = child_storm.shape
    npiece = storm_shift.shape[1]
    band_rows = crows // npiece
    nx, ny = lax.axis_size("gx"), lax.axis_size("gy")
    gathered = lax.all_to_all(
        storm_pieces(child_storm, npiece, devices), ("gx", "gy"), 0, 0, tiled=True
    )
    sources = storm_sources(storm_shift, nx, ny)
    storm_out = jnp.take_along_axis(gathered, sources[:, :, None], axis=0)
    dest_table = strip_dest.reshape(devices, -1)
    row_table = strip_row.reshape(devices, -1)
    target_table = strip_target.reshape(devices, -1)
    slots = dest_table.shape[1]
    my_dest = lax.dynamic_index_in_dim(dest_table, my_index, 0, keepdims=False)
    my_rows = lax.dynamic_index_in_dim(row_table, my_index, 0, keepdims=False)
    same_owner = my_dest[:, None] == my_dest[None, :]
    earlier = jnp.arange(slots)[None, :] < jnp.arange(slots)[:, None]
    rank = jnp.sum((same_owner & earlier).astype(jnp.int32), axis=1)
    slot_index = my_dest * CAP + rank
    send_select = (jnp.arange(devices * CAP)[:, None] == slot_index[None, :]).astype(jnp.float32)
    both_states = jnp.stack([parent_field, new_parent]).reshape(2, levels, -1, STRIP)
    picked = jnp.take(both_states, my_rows, axis=2)
    strip_values = jnp.moveaxis(picked, 2, 0).reshape(slots, -1)
    outgoing_strips = jnp.dot(
        send_select,
        strip_values,
        precision=lax.Precision.HIGHEST,
        preferred_element_type=jnp.float32,
    )
    strip_width = outgoing_strips.shape[1]
    outgoing = jnp.concatenate(
        [outgoing_strips.reshape(devices, -1), storm_out.reshape(devices, -1)], axis=1
    )
    arrived = lax.all_to_all(outgoing, ("gx", "gy"), split_axis=0, concat_axis=0, tiled=True)
    strip_part = CAP * strip_width
    incoming = arrived[:, :strip_part].reshape(devices * CAP, strip_width)
    child = storm_unpieces(
        arrived[:, strip_part:].reshape(devices, npiece, -1), levels, crows, widths
    )
    mine = dest_table == my_index
    rank_all = jnp.cumsum(mine.astype(jnp.int32), axis=1) - 1
    slot_ids = jnp.arange(CAP)
    hits = mine[:, None, :] & (rank_all[:, None, :] == slot_ids[None, :, None])
    chosen = jnp.sum(jnp.where(hits, target_table[:, None, :], 0), axis=2)
    target_rows = jnp.where(jnp.any(hits, axis=2), chosen, -1).reshape(-1)
    row_select = (jnp.arange(crows)[:, None] == target_rows[None, :]).astype(jnp.float32)
    coarse = jnp.dot(
        row_select, incoming, precision=lax.Precision.HIGHEST, preferred_element_type=jnp.float32
    )
    counts = jnp.sum(row_select, axis=1)
    boundary = jnp.einsum(
        "tald,de->alte",
        coarse.reshape(crows, 2, levels, STRIP),
        refine_table(STRIP),
        precision=lax.Precision.HIGHEST,
    )
    divisor = 1.0 + NUDGE * counts[None, :, None]
    factor = 1.0 + child_sppt.astype(jnp.float32)
    for substep in range(SUBSTEPS):
        weight = (substep + 1) / 3.0
        target_value = boundary[0] + weight * (boundary[1] - boundary[0])
        child = (
            child + factor * halo_tendency(child, wind_x, wind_y) + NUDGE * target_value
        ) / divisor
    return (new_parent, child)


def solution(mesh):
    placed = (
        P(None, "gx", "gy"),
        P("gx", "gy"),
        P(None, "gx", "gy"),
        P("gx", "gy"),
        P(),
        P(),
        P(),
        P(),
        P(),
    )
    return jax.shard_map(
        shards,
        mesh=mesh,
        in_specs=placed,
        out_specs=(P(None, "gx", "gy"), P(None, "gx", "gy")),
        check_vma=False,
    )
```

```python
import jax
import jax.numpy as jnp
from jax import lax
from jax.sharding import PartitionSpec as P

SUBSTEPS = 3
STRIP = 128
CAP = 2


KAPPA = 0.1
VERTICAL = 0.1
NUDGE = 0.5


def edge_halos(block):
    def swap(edge, axis, forward):
        count = lax.axis_size(axis)
        pairs = [(i, i + 1) for i in range(count - 1)]
        if not forward:
            pairs = [(target, source) for source, target in pairs]
        return lax.ppermute(edge, axis, pairs)

    before_x = swap(block[:, -1, :], "gx", True)
    after_x = swap(block[:, 0, :], "gx", False)
    before_y = swap(block[:, :, -1], "gy", True)
    after_y = swap(block[:, :, 0], "gy", False)
    return before_x, after_x, before_y, after_y


def halo_tendency(block, wind_x, wind_y):
    before_x, after_x, before_y, after_y = edge_halos(block)
    north = jnp.concatenate([block[:, 1:, :], after_x[:, None, :]], axis=1)
    south = jnp.concatenate([before_x[:, None, :], block[:, :-1, :]], axis=1)
    east = jnp.concatenate([block[:, :, 1:], after_y[:, :, None]], axis=2)
    west = jnp.concatenate([before_y[:, :, None], block[:, :, :-1]], axis=2)
    laplace = north + south + east + west - 4.0 * block
    return KAPPA * laplace - wind_x * (0.5 * (north - south)) - wind_y * (0.5 * (east - west))


def from_behind(value, axis, steps):
    count = lax.axis_size(axis)
    pairs = [(source, (source + steps) % count) for source in range(count)]
    return lax.ppermute(value, axis, pairs)


def storm_rows(child, storm_shift, nx, ny):
    levels, crows, widths = child.shape
    mine = lax.axis_index(("gx", "gy"))
    gathered = lax.all_to_all(child, ("gx", "gy"), 1, 1, tiled=True)
    piece = mine // (crows // storm_shift.shape[1])
    grid = gathered.reshape(levels, nx, ny, widths)
    grid = jnp.roll(grid, storm_shift[0, piece], axis=1)
    grid = jnp.roll(grid, storm_shift[1, piece], axis=2)
    return lax.all_to_all(grid.reshape(levels, crows, widths), ("gx", "gy"), 1, 1, tiled=True)


def refine_table(strip):
    coarse = jnp.arange(strip).astype(jnp.float32)
    finer = jnp.arange(3 * strip).astype(jnp.float32)
    position = jnp.clip((finer + 0.5) / 3.0 - 0.5, 0.0, strip - 1.0)
    return jnp.maximum(0.0, 1.0 - jnp.abs(position[None, :] - coarse[:, None]))


def vertical(field):
    upper = jnp.concatenate([field[1:], field[-1:]], axis=0)
    lower = jnp.concatenate([field[:1], field[:-1]], axis=0)
    return upper + lower - 2.0 * field


def shards(
    parent_field,
    parent_sppt,
    child_storm,
    child_sppt,
    wind,
    strip_dest,
    strip_row,
    strip_target,
    storm_shift,
):
    devices = lax.axis_size(("gx", "gy"))
    my_index = lax.axis_index(("gx", "gy"))
    wind_x = wind[0][:, None, None]
    wind_y = wind[1][:, None, None]
    new_parent = parent_field + (1.0 + parent_sppt.astype(jnp.float32)) * (
        halo_tendency(parent_field, wind_x, wind_y) + VERTICAL * vertical(parent_field)
    )
    levels, crows, widths = child_storm.shape
    npiece = storm_shift.shape[1]
    band_rows = crows // npiece
    nx, ny = lax.axis_size("gx"), lax.axis_size("gy")
    child = storm_rows(child_storm, storm_shift, nx, ny)
    dest_table = strip_dest.reshape(devices, -1)
    row_table = strip_row.reshape(devices, -1)
    target_table = strip_target.reshape(devices, -1)
    slots = dest_table.shape[1]
    my_dest = lax.dynamic_index_in_dim(dest_table, my_index, 0, keepdims=False)
    my_rows = lax.dynamic_index_in_dim(row_table, my_index, 0, keepdims=False)
    same_owner = my_dest[:, None] == my_dest[None, :]
    earlier = jnp.arange(slots)[None, :] < jnp.arange(slots)[:, None]
    rank = jnp.sum((same_owner & earlier).astype(jnp.int32), axis=1)
    slot_index = my_dest * CAP + rank
    send_select = (jnp.arange(devices * CAP)[:, None] == slot_index[None, :]).astype(jnp.float32)
    both_states = jnp.stack([parent_field, new_parent]).reshape(2, levels, -1, STRIP)
    picked = jnp.take(both_states, my_rows, axis=2)
    strip_values = jnp.moveaxis(picked, 2, 0).reshape(slots, -1)
    outgoing_strips = jnp.dot(
        send_select,
        strip_values,
        precision=lax.Precision.HIGHEST,
        preferred_element_type=jnp.float32,
    )
    incoming = lax.all_to_all(
        outgoing_strips, ("gx", "gy"), split_axis=0, concat_axis=0, tiled=True
    )
    mine = dest_table == my_index
    rank_all = jnp.cumsum(mine.astype(jnp.int32), axis=1) - 1
    slot_ids = jnp.arange(CAP)
    hits = mine[:, None, :] & (rank_all[:, None, :] == slot_ids[None, :, None])
    chosen = jnp.sum(jnp.where(hits, target_table[:, None, :], 0), axis=2)
    target_rows = jnp.where(jnp.any(hits, axis=2), chosen, -1).reshape(-1)
    row_select = (jnp.arange(crows)[:, None] == target_rows[None, :]).astype(jnp.float32)
    coarse = jnp.dot(
        row_select, incoming, precision=lax.Precision.HIGHEST, preferred_element_type=jnp.float32
    )
    counts = jnp.sum(row_select, axis=1)
    boundary = jnp.einsum(
        "tald,de->alte",
        coarse.reshape(crows, 2, levels, STRIP),
        refine_table(STRIP),
        precision=lax.Precision.HIGHEST,
    )
    divisor = 1.0 + NUDGE * counts[None, :, None]
    factor = 1.0 + child_sppt.astype(jnp.float32)
    for substep in range(SUBSTEPS):
        weight = (substep + 1) / 3.0
        target_value = boundary[0] + weight * (boundary[1] - boundary[0])
        child = (
            child + factor * halo_tendency(child, wind_x, wind_y) + NUDGE * target_value
        ) / divisor
    return (new_parent, child)


def solution(mesh):
    placed = (
        P(None, "gx", "gy"),
        P("gx", "gy"),
        P(None, "gx", "gy"),
        P("gx", "gy"),
        P(),
        P(),
        P(),
        P(),
        P(),
    )
    return jax.shard_map(
        shards,
        mesh=mesh,
        in_specs=placed,
        out_specs=(P(None, "gx", "gy"), P(None, "gx", "gy")),
        check_vma=False,
    )
```

```python
import jax
import jax.numpy as jnp
from jax import lax
from jax.sharding import PartitionSpec as P
from jax.experimental import pallas as pl
from jax.experimental.pallas import tpu as pltpu
import functools

SUBSTEPS = 3
STRIP = 128
CAP = 2


KAPPA = 0.1
VERTICAL = 0.1
NUDGE = 0.5


def edge_halos(block):
    def swap(edge, axis, forward):
        count = lax.axis_size(axis)
        pairs = [(i, i + 1) for i in range(count - 1)]
        if not forward:
            pairs = [(target, source) for source, target in pairs]
        return lax.ppermute(edge, axis, pairs)

    before_x = swap(block[:, -1, :], "gx", True)
    after_x = swap(block[:, 0, :], "gx", False)
    before_y = swap(block[:, :, -1], "gy", True)
    after_y = swap(block[:, :, 0], "gy", False)
    return before_x, after_x, before_y, after_y


def halo_tendency(block, wind_x, wind_y):
    before_x, after_x, before_y, after_y = edge_halos(block)
    north = jnp.concatenate([block[:, 1:, :], after_x[:, None, :]], axis=1)
    south = jnp.concatenate([before_x[:, None, :], block[:, :-1, :]], axis=1)
    east = jnp.concatenate([block[:, :, 1:], after_y[:, :, None]], axis=2)
    west = jnp.concatenate([before_y[:, :, None], block[:, :, :-1]], axis=2)
    laplace = north + south + east + west - 4.0 * block
    return KAPPA * laplace - wind_x * (0.5 * (north - south)) - wind_y * (0.5 * (east - west))


def from_behind(value, axis, steps):
    count = lax.axis_size(axis)
    pairs = [(source, (source + steps) % count) for source in range(count)]
    return lax.ppermute(value, axis, pairs)


def storm_rows(child, storm_shift, nx, ny):
    levels, crows, widths = child.shape
    mine = lax.axis_index(("gx", "gy"))
    gathered = lax.all_to_all(child, ("gx", "gy"), 1, 1, tiled=True)
    piece = mine // (crows // storm_shift.shape[1])
    grid = gathered.reshape(levels, nx, ny, widths)
    grid = jnp.roll(grid, storm_shift[0, piece], axis=1)
    grid = jnp.roll(grid, storm_shift[1, piece], axis=2)
    return lax.all_to_all(grid.reshape(levels, crows, widths), ("gx", "gy"), 1, 1, tiled=True)


def substep_kernel(weight, wind_ref, child_ref, bx_ref, ax_ref, by_ref, ay_ref, bound_ref,
                   factor_ref, divisor_ref, out_ref, first_row_ref, last_row_ref, first_col_ref, last_col_ref):
    levels, rows, cols = child_ref.shape
    row_id = lax.broadcasted_iota(jnp.int32, (rows, cols), 0)
    col_id = lax.broadcasted_iota(jnp.int32, (rows, cols), 1)
    factor = factor_ref[...]
    divisor = divisor_ref[...]
    for l in range(levels):
        c = child_ref[l]
        north = jnp.where(row_id == rows - 1, ax_ref[l:l + 1, :], pltpu.roll(c, rows - 1, 0))
        south = jnp.where(row_id == 0, bx_ref[l:l + 1, :], pltpu.roll(c, 1, 0))
        east = jnp.where(col_id == cols - 1, ay_ref[:, l:l + 1], pltpu.roll(c, cols - 1, 1))
        west = jnp.where(col_id == 0, by_ref[:, l:l + 1], pltpu.roll(c, 1, 1))
        laplace = north + south + east + west - 4.0 * c
        tend = KAPPA * laplace - wind_ref[0, l] * (0.5 * (north - south)) - wind_ref[1, l] * (0.5 * (east - west))
        b0 = bound_ref[0, l]
        target = b0 + weight * (bound_ref[1, l] - b0)
        new = (c + factor * tend + NUDGE * target) / divisor
        out_ref[l] = new
        first_row_ref[l:l + 1, :] = new[0:1, :]
        last_row_ref[l:l + 1, :] = new[rows - 1:rows, :]
        first_col_ref[:, l:l + 1] = new[:, 0:1]
        last_col_ref[:, l:l + 1] = new[:, cols - 1:cols]


def substep(weight, wind, child, bx, ax, by, ay, bound, factor, divisor):
    levels, rows, cols = child.shape
    vmem = pl.BlockSpec(memory_space=pltpu.VMEM)
    smem = pl.BlockSpec(memory_space=pltpu.SMEM)
    f32 = jnp.float32
    return pl.pallas_call(
        functools.partial(substep_kernel, weight),
        out_shape=(
            jax.ShapeDtypeStruct((levels, rows, cols), f32),
            jax.ShapeDtypeStruct((levels, cols), f32),
            jax.ShapeDtypeStruct((levels, cols), f32),
            jax.ShapeDtypeStruct((rows, levels), f32),
            jax.ShapeDtypeStruct((rows, levels), f32),
        ),
        in_specs=[smem] + [vmem] * 8,
        out_specs=(vmem,) * 5,
        cost_estimate=pl.CostEstimate(
            flops=30 * levels * rows * cols, transcendentals=0,
            bytes_accessed=4 * (4 * levels * rows * cols + 2 * rows * cols)),
    )(wind, child, bx, ax, by, ay, bound, factor, divisor)


def swap_edge(edge, axis, forward):
    count = lax.axis_size(axis)
    pairs = [(i, i + 1) for i in range(count - 1)]
    if not forward:
        pairs = [(target, source) for source, target in pairs]
    return lax.ppermute(edge, axis, pairs)


def refine_table(strip):
    coarse = jnp.arange(strip).astype(jnp.float32)
    finer = jnp.arange(3 * strip).astype(jnp.float32)
    position = jnp.clip((finer + 0.5) / 3.0 - 0.5, 0.0, strip - 1.0)
    return jnp.maximum(0.0, 1.0 - jnp.abs(position[None, :] - coarse[:, None]))


def vertical(field):
    upper = jnp.concatenate([field[1:], field[-1:]], axis=0)
    lower = jnp.concatenate([field[:1], field[:-1]], axis=0)
    return upper + lower - 2.0 * field


def shards(
    parent_field,
    parent_sppt,
    child_storm,
    child_sppt,
    wind,
    strip_dest,
    strip_row,
    strip_target,
    storm_shift,
):
    devices = lax.axis_size(("gx", "gy"))
    my_index = lax.axis_index(("gx", "gy"))
    wind_x = wind[0][:, None, None]
    wind_y = wind[1][:, None, None]
    new_parent = parent_field + (1.0 + parent_sppt.astype(jnp.float32)) * (
        halo_tendency(parent_field, wind_x, wind_y) + VERTICAL * vertical(parent_field)
    )
    levels, crows, widths = child_storm.shape
    npiece = storm_shift.shape[1]
    band_rows = crows // npiece
    nx, ny = lax.axis_size("gx"), lax.axis_size("gy")
    child = storm_rows(child_storm, storm_shift, nx, ny)
    dest_table = strip_dest.reshape(devices, -1)
    row_table = strip_row.reshape(devices, -1)
    target_table = strip_target.reshape(devices, -1)
    slots = dest_table.shape[1]
    my_dest = lax.dynamic_index_in_dim(dest_table, my_index, 0, keepdims=False)
    my_rows = lax.dynamic_index_in_dim(row_table, my_index, 0, keepdims=False)
    same_owner = my_dest[:, None] == my_dest[None, :]
    earlier = jnp.arange(slots)[None, :] < jnp.arange(slots)[:, None]
    rank = jnp.sum((same_owner & earlier).astype(jnp.int32), axis=1)
    slot_index = my_dest * CAP + rank
    send_select = (jnp.arange(devices * CAP)[:, None] == slot_index[None, :]).astype(jnp.float32)
    both_states = jnp.stack([parent_field, new_parent]).reshape(2, levels, -1, STRIP)
    picked = jnp.take(both_states, my_rows, axis=2)
    strip_values = jnp.moveaxis(picked, 2, 0).reshape(slots, -1)
    outgoing_strips = jnp.dot(
        send_select,
        strip_values,
        precision=lax.Precision.HIGHEST,
        preferred_element_type=jnp.float32,
    )
    incoming = lax.all_to_all(
        outgoing_strips, ("gx", "gy"), split_axis=0, concat_axis=0, tiled=True
    )
    mine = dest_table == my_index
    rank_all = jnp.cumsum(mine.astype(jnp.int32), axis=1) - 1
    slot_ids = jnp.arange(CAP)
    hits = mine[:, None, :] & (rank_all[:, None, :] == slot_ids[None, :, None])
    chosen = jnp.sum(jnp.where(hits, target_table[:, None, :], 0), axis=2)
    target_rows = jnp.where(jnp.any(hits, axis=2), chosen, -1).reshape(-1)
    row_select = (jnp.arange(crows)[:, None] == target_rows[None, :]).astype(jnp.float32)
    coarse = jnp.dot(
        row_select, incoming, precision=lax.Precision.HIGHEST, preferred_element_type=jnp.float32
    )
    counts = jnp.sum(row_select, axis=1)
    boundary = jnp.einsum(
        "tald,de->alte",
        coarse.reshape(crows, 2, levels, STRIP),
        refine_table(STRIP),
        precision=lax.Precision.HIGHEST,
    )
    divisor = jnp.broadcast_to(1.0 + NUDGE * counts[:, None], (crows, widths))
    factor = 1.0 + child_sppt.astype(jnp.float32)
    edges = (child[:, 0, :], child[:, -1, :], child[:, :, 0].T, child[:, :, -1].T)
    for substep_index in range(SUBSTEPS):
        first_row, last_row, first_col, last_col = edges
        before_x = swap_edge(last_row, "gx", True)
        after_x = swap_edge(first_row, "gx", False)
        before_y = swap_edge(last_col, "gy", True)
        after_y = swap_edge(first_col, "gy", False)
        weight = (substep_index + 1) / 3.0
        child, *edges = substep(
            weight, wind, child, before_x, after_x, before_y, after_y, boundary, factor, divisor
        )
    return (new_parent, child)


def solution(mesh):
    placed = (
        P(None, "gx", "gy"),
        P("gx", "gy"),
        P(None, "gx", "gy"),
        P("gx", "gy"),
        P(),
        P(),
        P(),
        P(),
        P(),
    )
    return jax.shard_map(
        shards,
        mesh=mesh,
        in_specs=placed,
        out_specs=(P(None, "gx", "gy"), P(None, "gx", "gy")),
        check_vma=False,
    )
```

```python
import jax
import jax.numpy as jnp
from jax import lax
from jax.sharding import PartitionSpec as P
from jax.experimental import pallas as pl
from jax.experimental.pallas import tpu as pltpu
import functools

SUBSTEPS = 3
STRIP = 128
CAP = 2


KAPPA = 0.1
VERTICAL = 0.1
NUDGE = 0.5


def edge_halos(block):
    def swap(edge, axis, forward):
        count = lax.axis_size(axis)
        pairs = [(i, i + 1) for i in range(count - 1)]
        if not forward:
            pairs = [(target, source) for source, target in pairs]
        return lax.ppermute(edge, axis, pairs)

    before_x = swap(block[:, -1, :], "gx", True)
    after_x = swap(block[:, 0, :], "gx", False)
    before_y = swap(block[:, :, -1], "gy", True)
    after_y = swap(block[:, :, 0], "gy", False)
    return before_x, after_x, before_y, after_y


def halo_tendency(block, wind_x, wind_y):
    before_x, after_x, before_y, after_y = edge_halos(block)
    north = jnp.concatenate([block[:, 1:, :], after_x[:, None, :]], axis=1)
    south = jnp.concatenate([before_x[:, None, :], block[:, :-1, :]], axis=1)
    east = jnp.concatenate([block[:, :, 1:], after_y[:, :, None]], axis=2)
    west = jnp.concatenate([before_y[:, :, None], block[:, :, :-1]], axis=2)
    laplace = north + south + east + west - 4.0 * block
    return KAPPA * laplace - wind_x * (0.5 * (north - south)) - wind_y * (0.5 * (east - west))


def from_behind(value, axis, steps):
    count = lax.axis_size(axis)
    pairs = [(source, (source + steps) % count) for source in range(count)]
    return lax.ppermute(value, axis, pairs)


def storm_rows(child, storm_shift, nx, ny):
    levels, crows, widths = child.shape
    mine = lax.axis_index(("gx", "gy"))
    gathered = lax.all_to_all(child, ("gx", "gy"), 1, 1, tiled=True)
    piece = mine // (crows // storm_shift.shape[1])
    grid = gathered.reshape(levels, nx, ny, widths)
    grid = jnp.roll(grid, storm_shift[0, piece], axis=1)
    grid = jnp.roll(grid, storm_shift[1, piece], axis=2)
    return lax.all_to_all(grid.reshape(levels, crows, widths), ("gx", "gy"), 1, 1, tiled=True)


def substep_kernel(weight, wind_ref, child_ref, bx_ref, ax_ref, by_ref, ay_ref, bound_ref,
                   factor_ref, divisor_ref, out_ref, first_row_ref, last_row_ref, first_col_ref, last_col_ref):
    levels, rows, cols = child_ref.shape
    row_id = lax.broadcasted_iota(jnp.int32, (rows, cols), 0)
    col_id = lax.broadcasted_iota(jnp.int32, (rows, cols), 1)
    factor = factor_ref[...]
    divisor = divisor_ref[...]
    for l in range(levels):
        c = child_ref[l]
        north = jnp.where(row_id == rows - 1, ax_ref[l:l + 1, :], pltpu.roll(c, rows - 1, 0))
        south = jnp.where(row_id == 0, bx_ref[l:l + 1, :], pltpu.roll(c, 1, 0))
        east = jnp.where(col_id == cols - 1, ay_ref[:, l:l + 1], pltpu.roll(c, cols - 1, 1))
        west = jnp.where(col_id == 0, by_ref[:, l:l + 1], pltpu.roll(c, 1, 1))
        laplace = north + south + east + west - 4.0 * c
        tend = KAPPA * laplace - wind_ref[0, l] * (0.5 * (north - south)) - wind_ref[1, l] * (0.5 * (east - west))
        b0 = bound_ref[0, l]
        target = b0 + weight * (bound_ref[1, l] - b0)
        new = (c + factor * tend + NUDGE * target) / divisor
        out_ref[l] = new
        first_row_ref[l:l + 1, :] = new[0:1, :]
        last_row_ref[l:l + 1, :] = new[rows - 1:rows, :]
        first_col_ref[:, l:l + 1] = new[:, 0:1]
        last_col_ref[:, l:l + 1] = new[:, cols - 1:cols]


def substep(weight, wind, child, bx, ax, by, ay, bound, factor, divisor):
    levels, rows, cols = child.shape
    vmem = pl.BlockSpec(memory_space=pltpu.VMEM)
    smem = pl.BlockSpec(memory_space=pltpu.SMEM)
    f32 = jnp.float32
    return pl.pallas_call(
        functools.partial(substep_kernel, weight),
        out_shape=(
            jax.ShapeDtypeStruct((levels, rows, cols), f32),
            jax.ShapeDtypeStruct((levels, cols), f32),
            jax.ShapeDtypeStruct((levels, cols), f32),
            jax.ShapeDtypeStruct((rows, levels), f32),
            jax.ShapeDtypeStruct((rows, levels), f32),
        ),
        in_specs=[smem] + [vmem] * 8,
        out_specs=(vmem,) * 5,
        cost_estimate=pl.CostEstimate(
            flops=30 * levels * rows * cols, transcendentals=0,
            bytes_accessed=4 * (4 * levels * rows * cols + 2 * rows * cols)),
    )(wind, child, bx, ax, by, ay, bound, factor, divisor)


def swap_edge(edge, axis, forward):
    count = lax.axis_size(axis)
    pairs = [(i, i + 1) for i in range(count - 1)]
    if not forward:
        pairs = [(target, source) for source, target in pairs]
    return lax.ppermute(edge, axis, pairs)


def refine_table(strip):
    coarse = jnp.arange(strip).astype(jnp.float32)
    finer = jnp.arange(3 * strip).astype(jnp.float32)
    position = jnp.clip((finer + 0.5) / 3.0 - 0.5, 0.0, strip - 1.0)
    return jnp.maximum(0.0, 1.0 - jnp.abs(position[None, :] - coarse[:, None]))


def vertical(field):
    upper = jnp.concatenate([field[1:], field[-1:]], axis=0)
    lower = jnp.concatenate([field[:1], field[:-1]], axis=0)
    return upper + lower - 2.0 * field


def shards(
    parent_field,
    parent_sppt,
    child_storm,
    child_sppt,
    wind,
    strip_dest,
    strip_row,
    strip_target,
    storm_shift,
):
    devices = lax.axis_size(("gx", "gy"))
    my_index = lax.axis_index(("gx", "gy"))
    wind_x = wind[0][:, None, None]
    wind_y = wind[1][:, None, None]
    new_parent = parent_field + (1.0 + parent_sppt.astype(jnp.float32)) * (
        halo_tendency(parent_field, wind_x, wind_y) + VERTICAL * vertical(parent_field)
    )
    levels, crows, widths = child_storm.shape
    npiece = storm_shift.shape[1]
    band_rows = crows // npiece
    nx, ny = lax.axis_size("gx"), lax.axis_size("gy")
    child = storm_rows(child_storm, storm_shift, nx, ny)
    dest_table = strip_dest.reshape(devices, -1)
    row_table = strip_row.reshape(devices, -1)
    target_table = strip_target.reshape(devices, -1)
    slots = dest_table.shape[1]
    my_dest = lax.dynamic_index_in_dim(dest_table, my_index, 0, keepdims=False)
    my_rows = lax.dynamic_index_in_dim(row_table, my_index, 0, keepdims=False)
    same_owner = my_dest[:, None] == my_dest[None, :]
    earlier = jnp.arange(slots)[None, :] < jnp.arange(slots)[:, None]
    rank = jnp.sum((same_owner & earlier).astype(jnp.int32), axis=1)
    slot_index = my_dest * CAP + rank
    send_select = (jnp.arange(devices * CAP)[:, None] == slot_index[None, :]).astype(jnp.float32)
    both_states = jnp.stack([parent_field, new_parent]).reshape(2, levels, -1, STRIP)
    picked = jnp.take(both_states, my_rows, axis=2)
    strip_values = jnp.moveaxis(picked, 2, 0).reshape(slots, -1)
    outgoing_strips = jnp.dot(
        send_select,
        strip_values,
        precision=lax.Precision.HIGHEST,
        preferred_element_type=jnp.float32,
    )
    child, outgoing_strips = lax.optimization_barrier((child, outgoing_strips))
    incoming = lax.all_to_all(
        outgoing_strips, ("gx", "gy"), split_axis=0, concat_axis=0, tiled=True
    )
    mine = dest_table == my_index
    rank_all = jnp.cumsum(mine.astype(jnp.int32), axis=1) - 1
    slot_ids = jnp.arange(CAP)
    hits = mine[:, None, :] & (rank_all[:, None, :] == slot_ids[None, :, None])
    chosen = jnp.sum(jnp.where(hits, target_table[:, None, :], 0), axis=2)
    target_rows = jnp.where(jnp.any(hits, axis=2), chosen, -1).reshape(-1)
    row_select = (jnp.arange(crows)[:, None] == target_rows[None, :]).astype(jnp.float32)
    coarse = jnp.dot(
        row_select, incoming, precision=lax.Precision.HIGHEST, preferred_element_type=jnp.float32
    )
    counts = jnp.sum(row_select, axis=1)
    boundary = jnp.einsum(
        "tald,de->alte",
        coarse.reshape(crows, 2, levels, STRIP),
        refine_table(STRIP),
        precision=lax.Precision.HIGHEST,
    )
    divisor = jnp.broadcast_to(1.0 + NUDGE * counts[:, None], (crows, widths))
    factor = 1.0 + child_sppt.astype(jnp.float32)
    edges = (child[:, 0, :], child[:, -1, :], child[:, :, 0].T, child[:, :, -1].T)
    for substep_index in range(SUBSTEPS):
        first_row, last_row, first_col, last_col = edges
        before_x = swap_edge(last_row, "gx", True)
        after_x = swap_edge(first_row, "gx", False)
        before_y = swap_edge(last_col, "gy", True)
        after_y = swap_edge(first_col, "gy", False)
        weight = (substep_index + 1) / 3.0
        child, *edges = substep(
            weight, wind, child, before_x, after_x, before_y, after_y, boundary, factor, divisor
        )
    return (new_parent, child)


def solution(mesh):
    placed = (
        P(None, "gx", "gy"),
        P("gx", "gy"),
        P(None, "gx", "gy"),
        P("gx", "gy"),
        P(),
        P(),
        P(),
        P(),
        P(),
    )
    return jax.shard_map(
        shards,
        mesh=mesh,
        in_specs=placed,
        out_specs=(P(None, "gx", "gy"), P(None, "gx", "gy")),
        check_vma=False,
    )
```

```python
import jax
import jax.numpy as jnp
from jax import lax
from jax.sharding import PartitionSpec as P
from jax.experimental import pallas as pl
from jax.experimental.pallas import tpu as pltpu
import functools

SUBSTEPS = 3
STRIP = 128
CAP = 2


KAPPA = 0.1
VERTICAL = 0.1
NUDGE = 0.5


def edge_halos(block):
    def swap(edge, axis, forward):
        count = lax.axis_size(axis)
        pairs = [(i, i + 1) for i in range(count - 1)]
        if not forward:
            pairs = [(target, source) for source, target in pairs]
        return lax.ppermute(edge, axis, pairs)

    before_x = swap(block[:, -1, :], "gx", True)
    after_x = swap(block[:, 0, :], "gx", False)
    before_y = swap(block[:, :, -1], "gy", True)
    after_y = swap(block[:, :, 0], "gy", False)
    return before_x, after_x, before_y, after_y


def halo_tendency(block, wind_x, wind_y):
    before_x, after_x, before_y, after_y = edge_halos(block)
    north = jnp.concatenate([block[:, 1:, :], after_x[:, None, :]], axis=1)
    south = jnp.concatenate([before_x[:, None, :], block[:, :-1, :]], axis=1)
    east = jnp.concatenate([block[:, :, 1:], after_y[:, :, None]], axis=2)
    west = jnp.concatenate([before_y[:, :, None], block[:, :, :-1]], axis=2)
    laplace = north + south + east + west - 4.0 * block
    return KAPPA * laplace - wind_x * (0.5 * (north - south)) - wind_y * (0.5 * (east - west))


def from_behind(value, axis, steps):
    count = lax.axis_size(axis)
    pairs = [(source, (source + steps) % count) for source in range(count)]
    return lax.ppermute(value, axis, pairs)


def storm_rows(child, storm_shift, nx, ny):
    levels, crows, widths = child.shape
    mine = lax.axis_index(("gx", "gy"))
    gathered = lax.all_to_all(child, ("gx", "gy"), 1, 1, tiled=True)
    piece = mine // (crows // storm_shift.shape[1])
    grid = gathered.reshape(levels, nx, ny, widths)
    grid = jnp.roll(grid, storm_shift[0, piece], axis=1)
    grid = jnp.roll(grid, storm_shift[1, piece], axis=2)
    return lax.all_to_all(grid.reshape(levels, crows, widths), ("gx", "gy"), 1, 1, tiled=True)


def substep_kernel(weight, wind_ref, child_ref, bx_ref, ax_ref, by_ref, ay_ref, bound_ref,
                   factor_ref, divisor_ref, out_ref, first_row_ref, last_row_ref, first_col_ref, last_col_ref):
    levels, rows, cols = child_ref.shape
    row_id = lax.broadcasted_iota(jnp.int32, (rows, cols), 0)
    col_id = lax.broadcasted_iota(jnp.int32, (rows, cols), 1)
    factor = factor_ref[...]
    divisor = divisor_ref[...]
    for l in range(levels):
        c = child_ref[l]
        north = jnp.where(row_id == rows - 1, ax_ref[l:l + 1, :], pltpu.roll(c, rows - 1, 0))
        south = jnp.where(row_id == 0, bx_ref[l:l + 1, :], pltpu.roll(c, 1, 0))
        east = jnp.where(col_id == cols - 1, ay_ref[:, l:l + 1], pltpu.roll(c, cols - 1, 1))
        west = jnp.where(col_id == 0, by_ref[:, l:l + 1], pltpu.roll(c, 1, 1))
        laplace = north + south + east + west - 4.0 * c
        tend = KAPPA * laplace - wind_ref[0, l] * (0.5 * (north - south)) - wind_ref[1, l] * (0.5 * (east - west))
        b0 = bound_ref[0, l]
        target = b0 + weight * (bound_ref[1, l] - b0)
        new = (c + factor * tend + NUDGE * target) / divisor
        out_ref[l] = new
        first_row_ref[l:l + 1, :] = new[0:1, :]
        last_row_ref[l:l + 1, :] = new[rows - 1:rows, :]
        first_col_ref[:, l:l + 1] = new[:, 0:1]
        last_col_ref[:, l:l + 1] = new[:, cols - 1:cols]


def substep(weight, wind, child, bx, ax, by, ay, bound, factor, divisor):
    levels, rows, cols = child.shape
    vmem = pl.BlockSpec(memory_space=pltpu.VMEM)
    smem = pl.BlockSpec(memory_space=pltpu.SMEM)
    f32 = jnp.float32
    return pl.pallas_call(
        functools.partial(substep_kernel, weight),
        out_shape=(
            jax.ShapeDtypeStruct((levels, rows, cols), f32),
            jax.ShapeDtypeStruct((levels, cols), f32),
            jax.ShapeDtypeStruct((levels, cols), f32),
            jax.ShapeDtypeStruct((rows, levels), f32),
            jax.ShapeDtypeStruct((rows, levels), f32),
        ),
        in_specs=[smem] + [vmem] * 8,
        out_specs=(vmem,) * 5,
        cost_estimate=pl.CostEstimate(
            flops=30 * levels * rows * cols, transcendentals=0,
            bytes_accessed=4 * (4 * levels * rows * cols + 2 * rows * cols)),
    )(wind, child, bx, ax, by, ay, bound, factor, divisor)


def swap_edge(edge, axis, forward):
    count = lax.axis_size(axis)
    pairs = [(i, i + 1) for i in range(count - 1)]
    if not forward:
        pairs = [(target, source) for source, target in pairs]
    return lax.ppermute(edge, axis, pairs)


def refine_table(strip):
    coarse = jnp.arange(strip).astype(jnp.float32)
    finer = jnp.arange(3 * strip).astype(jnp.float32)
    position = jnp.clip((finer + 0.5) / 3.0 - 0.5, 0.0, strip - 1.0)
    return jnp.maximum(0.0, 1.0 - jnp.abs(position[None, :] - coarse[:, None]))


def vertical(field):
    upper = jnp.concatenate([field[1:], field[-1:]], axis=0)
    lower = jnp.concatenate([field[:1], field[:-1]], axis=0)
    return upper + lower - 2.0 * field


def shards(
    parent_field,
    parent_sppt,
    child_storm,
    child_sppt,
    wind,
    strip_dest,
    strip_row,
    strip_target,
    storm_shift,
):
    devices = lax.axis_size(("gx", "gy"))
    my_index = lax.axis_index(("gx", "gy"))
    wind_x = wind[0][:, None, None]
    wind_y = wind[1][:, None, None]
    new_parent = parent_field + (1.0 + parent_sppt.astype(jnp.float32)) * (
        halo_tendency(parent_field, wind_x, wind_y) + VERTICAL * vertical(parent_field)
    )
    levels, crows, widths = child_storm.shape
    npiece = storm_shift.shape[1]
    band_rows = crows // npiece
    nx, ny = lax.axis_size("gx"), lax.axis_size("gy")
    child = storm_rows(child_storm, storm_shift, nx, ny)
    dest_table = strip_dest.reshape(devices, -1)
    row_table = strip_row.reshape(devices, -1)
    target_table = strip_target.reshape(devices, -1)
    slots = dest_table.shape[1]
    my_dest = lax.dynamic_index_in_dim(dest_table, my_index, 0, keepdims=False)
    my_rows = lax.dynamic_index_in_dim(row_table, my_index, 0, keepdims=False)
    same_owner = my_dest[:, None] == my_dest[None, :]
    earlier = jnp.arange(slots)[None, :] < jnp.arange(slots)[:, None]
    rank = jnp.sum((same_owner & earlier).astype(jnp.int32), axis=1)
    slot_index = my_dest * CAP + rank
    send_select = (jnp.arange(devices * CAP)[:, None] == slot_index[None, :]).astype(jnp.float32)
    both_states = jnp.stack([parent_field, new_parent]).reshape(2, levels, -1, STRIP)
    picked = jnp.take(both_states, my_rows, axis=2)
    strip_values = jnp.moveaxis(picked, 2, 0).reshape(slots, -1)
    outgoing_strips = jnp.dot(
        send_select,
        strip_values,
        precision=lax.Precision.HIGHEST,
        preferred_element_type=jnp.float32,
    )
    _, outgoing_strips = lax.optimization_barrier((child[0, 0, :], outgoing_strips))
    incoming = lax.all_to_all(
        outgoing_strips, ("gx", "gy"), split_axis=0, concat_axis=0, tiled=True
    )
    mine = dest_table == my_index
    rank_all = jnp.cumsum(mine.astype(jnp.int32), axis=1) - 1
    slot_ids = jnp.arange(CAP)
    hits = mine[:, None, :] & (rank_all[:, None, :] == slot_ids[None, :, None])
    chosen = jnp.sum(jnp.where(hits, target_table[:, None, :], 0), axis=2)
    target_rows = jnp.where(jnp.any(hits, axis=2), chosen, -1).reshape(-1)
    row_select = (jnp.arange(crows)[:, None] == target_rows[None, :]).astype(jnp.float32)
    coarse = jnp.dot(
        row_select, incoming, precision=lax.Precision.HIGHEST, preferred_element_type=jnp.float32
    )
    counts = jnp.sum(row_select, axis=1)
    boundary = jnp.einsum(
        "tald,de->alte",
        coarse.reshape(crows, 2, levels, STRIP),
        refine_table(STRIP),
        precision=lax.Precision.HIGHEST,
    )
    divisor = jnp.broadcast_to(1.0 + NUDGE * counts[:, None], (crows, widths))
    factor = 1.0 + child_sppt.astype(jnp.float32)
    edges = (child[:, 0, :], child[:, -1, :], child[:, :, 0].T, child[:, :, -1].T)
    for substep_index in range(SUBSTEPS):
        first_row, last_row, first_col, last_col = edges
        before_x = swap_edge(last_row, "gx", True)
        after_x = swap_edge(first_row, "gx", False)
        before_y = swap_edge(last_col, "gy", True)
        after_y = swap_edge(first_col, "gy", False)
        weight = (substep_index + 1) / 3.0
        child, *edges = substep(
            weight, wind, child, before_x, after_x, before_y, after_y, boundary, factor, divisor
        )
    return (new_parent, child)


def solution(mesh):
    placed = (
        P(None, "gx", "gy"),
        P("gx", "gy"),
        P(None, "gx", "gy"),
        P("gx", "gy"),
        P(),
        P(),
        P(),
        P(),
        P(),
    )
    return jax.shard_map(
        shards,
        mesh=mesh,
        in_specs=placed,
        out_specs=(P(None, "gx", "gy"), P(None, "gx", "gy")),
        check_vma=False,
    )
```

```python
import jax
import jax.numpy as jnp
from jax import lax
from jax.sharding import PartitionSpec as P
from jax.experimental import pallas as pl
from jax.experimental.pallas import tpu as pltpu
import functools

SUBSTEPS = 3
STRIP = 128
CAP = 2


KAPPA = 0.1
VERTICAL = 0.1
NUDGE = 0.5


def edge_halos(block):
    def swap(edge, axis, forward):
        count = lax.axis_size(axis)
        pairs = [(i, i + 1) for i in range(count - 1)]
        if not forward:
            pairs = [(target, source) for source, target in pairs]
        return lax.ppermute(edge, axis, pairs)

    before_x = swap(block[:, -1, :], "gx", True)
    after_x = swap(block[:, 0, :], "gx", False)
    before_y = swap(block[:, :, -1], "gy", True)
    after_y = swap(block[:, :, 0], "gy", False)
    return before_x, after_x, before_y, after_y


def halo_tendency(block, wind_x, wind_y):
    before_x, after_x, before_y, after_y = edge_halos(block)
    north = jnp.concatenate([block[:, 1:, :], after_x[:, None, :]], axis=1)
    south = jnp.concatenate([before_x[:, None, :], block[:, :-1, :]], axis=1)
    east = jnp.concatenate([block[:, :, 1:], after_y[:, :, None]], axis=2)
    west = jnp.concatenate([before_y[:, :, None], block[:, :, :-1]], axis=2)
    laplace = north + south + east + west - 4.0 * block
    return KAPPA * laplace - wind_x * (0.5 * (north - south)) - wind_y * (0.5 * (east - west))


def from_behind(value, axis, steps):
    count = lax.axis_size(axis)
    pairs = [(source, (source + steps) % count) for source in range(count)]
    return lax.ppermute(value, axis, pairs)


def storm_rows(child, storm_shift, nx, ny):
    levels, crows, widths = child.shape
    mine = lax.axis_index(("gx", "gy"))
    gathered = lax.all_to_all(child, ("gx", "gy"), 1, 1, tiled=True)
    piece = mine // (crows // storm_shift.shape[1])
    grid = gathered.reshape(levels, nx, ny, widths)
    grid = jnp.roll(grid, storm_shift[0, piece], axis=1)
    grid = jnp.roll(grid, storm_shift[1, piece], axis=2)
    return lax.all_to_all(grid.reshape(levels, crows, widths), ("gx", "gy"), 1, 1, tiled=True)


def substep_kernel(weight, wind_ref, child_ref, bx_ref, ax_ref, by_ref, ay_ref, bound_ref,
                   factor_ref, divisor_ref, out_ref, first_row_ref, last_row_ref, first_col_ref, last_col_ref):
    levels, rows, cols = child_ref.shape
    row_id = lax.broadcasted_iota(jnp.int32, (rows, cols), 0)
    col_id = lax.broadcasted_iota(jnp.int32, (rows, cols), 1)
    factor = factor_ref[...]
    divisor = divisor_ref[...]
    for l in range(levels):
        c = child_ref[l]
        north = jnp.where(row_id == rows - 1, ax_ref[l:l + 1, :], pltpu.roll(c, rows - 1, 0))
        south = jnp.where(row_id == 0, bx_ref[l:l + 1, :], pltpu.roll(c, 1, 0))
        east = jnp.where(col_id == cols - 1, ay_ref[:, l:l + 1], pltpu.roll(c, cols - 1, 1))
        west = jnp.where(col_id == 0, by_ref[:, l:l + 1], pltpu.roll(c, 1, 1))
        laplace = north + south + east + west - 4.0 * c
        tend = KAPPA * laplace - wind_ref[0, l] * (0.5 * (north - south)) - wind_ref[1, l] * (0.5 * (east - west))
        b0 = bound_ref[0, l]
        target = b0 + weight * (bound_ref[1, l] - b0)
        new = (c + factor * tend + NUDGE * target) / divisor
        out_ref[l] = new
        first_row_ref[l:l + 1, :] = new[0:1, :]
        last_row_ref[l:l + 1, :] = new[rows - 1:rows, :]
        first_col_ref[:, l:l + 1] = new[:, 0:1]
        last_col_ref[:, l:l + 1] = new[:, cols - 1:cols]


def substep(weight, wind, child, bx, ax, by, ay, bound, factor, divisor):
    levels, rows, cols = child.shape
    vmem = pl.BlockSpec(memory_space=pltpu.VMEM)
    smem = pl.BlockSpec(memory_space=pltpu.SMEM)
    f32 = jnp.float32
    return pl.pallas_call(
        functools.partial(substep_kernel, weight),
        out_shape=(
            jax.ShapeDtypeStruct((levels, rows, cols), f32),
            jax.ShapeDtypeStruct((levels, cols), f32),
            jax.ShapeDtypeStruct((levels, cols), f32),
            jax.ShapeDtypeStruct((rows, levels), f32),
            jax.ShapeDtypeStruct((rows, levels), f32),
        ),
        in_specs=[smem] + [vmem] * 8,
        out_specs=(vmem,) * 5,
        cost_estimate=pl.CostEstimate(
            flops=30 * levels * rows * cols, transcendentals=0,
            bytes_accessed=4 * (4 * levels * rows * cols + 2 * rows * cols)),
    )(wind, child, bx, ax, by, ay, bound, factor, divisor)


def swap_edge(edge, axis, forward):
    count = lax.axis_size(axis)
    pairs = [(i, i + 1) for i in range(count - 1)]
    if not forward:
        pairs = [(target, source) for source, target in pairs]
    return lax.ppermute(edge, axis, pairs)


def refine_table(strip):
    coarse = jnp.arange(strip).astype(jnp.float32)
    finer = jnp.arange(3 * strip).astype(jnp.float32)
    position = jnp.clip((finer + 0.5) / 3.0 - 0.5, 0.0, strip - 1.0)
    return jnp.maximum(0.0, 1.0 - jnp.abs(position[None, :] - coarse[:, None]))


def vertical(field):
    upper = jnp.concatenate([field[1:], field[-1:]], axis=0)
    lower = jnp.concatenate([field[:1], field[:-1]], axis=0)
    return upper + lower - 2.0 * field


def shards(
    parent_field,
    parent_sppt,
    child_storm,
    child_sppt,
    wind,
    strip_dest,
    strip_row,
    strip_target,
    storm_shift,
):
    devices = lax.axis_size(("gx", "gy"))
    my_index = lax.axis_index(("gx", "gy"))
    wind_x = wind[0][:, None, None]
    wind_y = wind[1][:, None, None]
    new_parent = parent_field + (1.0 + parent_sppt.astype(jnp.float32)) * (
        halo_tendency(parent_field, wind_x, wind_y) + VERTICAL * vertical(parent_field)
    )
    levels, crows, widths = child_storm.shape
    npiece = storm_shift.shape[1]
    band_rows = crows // npiece
    nx, ny = lax.axis_size("gx"), lax.axis_size("gy")
    child = storm_rows(child_storm, storm_shift, nx, ny)
    dest_table = strip_dest.reshape(devices, -1)
    row_table = strip_row.reshape(devices, -1)
    target_table = strip_target.reshape(devices, -1)
    slots = dest_table.shape[1]
    my_dest = lax.dynamic_index_in_dim(dest_table, my_index, 0, keepdims=False)
    my_rows = lax.dynamic_index_in_dim(row_table, my_index, 0, keepdims=False)
    same_owner = my_dest[:, None] == my_dest[None, :]
    earlier = jnp.arange(slots)[None, :] < jnp.arange(slots)[:, None]
    rank = jnp.sum((same_owner & earlier).astype(jnp.int32), axis=1)
    slot_index = my_dest * CAP + rank
    send_select = (jnp.arange(devices * CAP)[:, None] == slot_index[None, :]).astype(jnp.float32)
    both_states = jnp.stack([parent_field, new_parent]).reshape(2, levels, -1, STRIP)
    picked = jnp.take(both_states, my_rows, axis=2)
    strip_values = jnp.moveaxis(picked, 2, 0).reshape(slots, -1)
    outgoing_strips = jnp.dot(
        send_select,
        strip_values,
        precision=lax.Precision.HIGHEST,
        preferred_element_type=jnp.float32,
    )
    outgoing_strips = outgoing_strips + 0.0 * child[0, 0, 0]
    incoming = lax.all_to_all(
        outgoing_strips, ("gx", "gy"), split_axis=0, concat_axis=0, tiled=True
    )
    mine = dest_table == my_index
    rank_all = jnp.cumsum(mine.astype(jnp.int32), axis=1) - 1
    slot_ids = jnp.arange(CAP)
    hits = mine[:, None, :] & (rank_all[:, None, :] == slot_ids[None, :, None])
    chosen = jnp.sum(jnp.where(hits, target_table[:, None, :], 0), axis=2)
    target_rows = jnp.where(jnp.any(hits, axis=2), chosen, -1).reshape(-1)
    row_select = (jnp.arange(crows)[:, None] == target_rows[None, :]).astype(jnp.float32)
    coarse = jnp.dot(
        row_select, incoming, precision=lax.Precision.HIGHEST, preferred_element_type=jnp.float32
    )
    counts = jnp.sum(row_select, axis=1)
    boundary = jnp.einsum(
        "tald,de->alte",
        coarse.reshape(crows, 2, levels, STRIP),
        refine_table(STRIP),
        precision=lax.Precision.HIGHEST,
    )
    divisor = jnp.broadcast_to(1.0 + NUDGE * counts[:, None], (crows, widths))
    factor = 1.0 + child_sppt.astype(jnp.float32)
    edges = (child[:, 0, :], child[:, -1, :], child[:, :, 0].T, child[:, :, -1].T)
    for substep_index in range(SUBSTEPS):
        first_row, last_row, first_col, last_col = edges
        before_x = swap_edge(last_row, "gx", True)
        after_x = swap_edge(first_row, "gx", False)
        before_y = swap_edge(last_col, "gy", True)
        after_y = swap_edge(first_col, "gy", False)
        weight = (substep_index + 1) / 3.0
        child, *edges = substep(
            weight, wind, child, before_x, after_x, before_y, after_y, boundary, factor, divisor
        )
    return (new_parent, child)


def solution(mesh):
    placed = (
        P(None, "gx", "gy"),
        P("gx", "gy"),
        P(None, "gx", "gy"),
        P("gx", "gy"),
        P(),
        P(),
        P(),
        P(),
        P(),
    )
    return jax.shard_map(
        shards,
        mesh=mesh,
        in_specs=placed,
        out_specs=(P(None, "gx", "gy"), P(None, "gx", "gy")),
        check_vma=False,
    )
```

```python
import jax
import jax.numpy as jnp
from jax import lax
from jax.sharding import PartitionSpec as P
from jax.experimental import pallas as pl
from jax.experimental.pallas import tpu as pltpu
import functools

SUBSTEPS = 3
STRIP = 128
CAP = 2


KAPPA = 0.1
VERTICAL = 0.1
NUDGE = 0.5


def edge_halos(block):
    def swap(edge, axis, forward):
        count = lax.axis_size(axis)
        pairs = [(i, i + 1) for i in range(count - 1)]
        if not forward:
            pairs = [(target, source) for source, target in pairs]
        return lax.ppermute(edge, axis, pairs)

    before_x = swap(block[:, -1, :], "gx", True)
    after_x = swap(block[:, 0, :], "gx", False)
    before_y = swap(block[:, :, -1], "gy", True)
    after_y = swap(block[:, :, 0], "gy", False)
    return before_x, after_x, before_y, after_y


def halo_tendency(block, wind_x, wind_y):
    before_x, after_x, before_y, after_y = edge_halos(block)
    north = jnp.concatenate([block[:, 1:, :], after_x[:, None, :]], axis=1)
    south = jnp.concatenate([before_x[:, None, :], block[:, :-1, :]], axis=1)
    east = jnp.concatenate([block[:, :, 1:], after_y[:, :, None]], axis=2)
    west = jnp.concatenate([before_y[:, :, None], block[:, :, :-1]], axis=2)
    laplace = north + south + east + west - 4.0 * block
    return KAPPA * laplace - wind_x * (0.5 * (north - south)) - wind_y * (0.5 * (east - west))


def from_behind(value, axis, steps):
    count = lax.axis_size(axis)
    pairs = [(source, (source + steps) % count) for source in range(count)]
    return lax.ppermute(value, axis, pairs)


def storm_rows(child, storm_shift, nx, ny):
    levels, crows, widths = child.shape
    mine = lax.axis_index(("gx", "gy"))
    gathered = lax.all_to_all(child, ("gx", "gy"), 1, 1, tiled=True)
    piece = mine // (crows // storm_shift.shape[1])
    grid = gathered.reshape(levels, nx, ny, widths)
    grid = jnp.roll(grid, storm_shift[0, piece], axis=1)
    grid = jnp.roll(grid, storm_shift[1, piece], axis=2)
    return lax.all_to_all(grid.reshape(levels, crows, widths), ("gx", "gy"), 1, 1, tiled=True)


def substep_kernel(weight, wind_ref, child_ref, bx_ref, ax_ref, by_ref, ay_ref, bound_ref,
                   factor_ref, divisor_ref, out_ref, first_row_ref, last_row_ref, first_col_ref, last_col_ref):
    levels, rows, cols = child_ref.shape
    row_id = lax.broadcasted_iota(jnp.int32, (rows, cols), 0)
    col_id = lax.broadcasted_iota(jnp.int32, (rows, cols), 1)
    factor = factor_ref[...]
    divisor = divisor_ref[...]
    for l in range(levels):
        c = child_ref[l]
        north = jnp.where(row_id == rows - 1, ax_ref[l:l + 1, :], pltpu.roll(c, rows - 1, 0))
        south = jnp.where(row_id == 0, bx_ref[l:l + 1, :], pltpu.roll(c, 1, 0))
        east = jnp.where(col_id == cols - 1, ay_ref[:, l:l + 1], pltpu.roll(c, cols - 1, 1))
        west = jnp.where(col_id == 0, by_ref[:, l:l + 1], pltpu.roll(c, 1, 1))
        laplace = north + south + east + west - 4.0 * c
        tend = KAPPA * laplace - wind_ref[0, l] * (0.5 * (north - south)) - wind_ref[1, l] * (0.5 * (east - west))
        b0 = bound_ref[0, l]
        target = b0 + weight * (bound_ref[1, l] - b0)
        new = (c + factor * tend + NUDGE * target) / divisor
        out_ref[l] = new
        first_row_ref[l:l + 1, :] = new[0:1, :]
        last_row_ref[l:l + 1, :] = new[rows - 1:rows, :]
        first_col_ref[:, l:l + 1] = new[:, 0:1]
        last_col_ref[:, l:l + 1] = new[:, cols - 1:cols]


def substep(weight, wind, child, bx, ax, by, ay, bound, factor, divisor):
    levels, rows, cols = child.shape
    vmem = pl.BlockSpec(memory_space=pltpu.VMEM)
    smem = pl.BlockSpec(memory_space=pltpu.SMEM)
    f32 = jnp.float32
    return pl.pallas_call(
        functools.partial(substep_kernel, weight),
        out_shape=(
            jax.ShapeDtypeStruct((levels, rows, cols), f32),
            jax.ShapeDtypeStruct((levels, cols), f32),
            jax.ShapeDtypeStruct((levels, cols), f32),
            jax.ShapeDtypeStruct((rows, levels), f32),
            jax.ShapeDtypeStruct((rows, levels), f32),
        ),
        in_specs=[smem] + [vmem] * 8,
        out_specs=(vmem,) * 5,
        cost_estimate=pl.CostEstimate(
            flops=30 * levels * rows * cols, transcendentals=0,
            bytes_accessed=4 * (4 * levels * rows * cols + 2 * rows * cols)),
    )(wind, child, bx, ax, by, ay, bound, factor, divisor)


def swap_edge(edge, axis, forward):
    count = lax.axis_size(axis)
    pairs = [(i, i + 1) for i in range(count - 1)]
    if not forward:
        pairs = [(target, source) for source, target in pairs]
    return lax.ppermute(edge, axis, pairs)


def refine_table(strip):
    coarse = jnp.arange(strip).astype(jnp.float32)
    finer = jnp.arange(3 * strip).astype(jnp.float32)
    position = jnp.clip((finer + 0.5) / 3.0 - 0.5, 0.0, strip - 1.0)
    return jnp.maximum(0.0, 1.0 - jnp.abs(position[None, :] - coarse[:, None]))


def vertical(field):
    upper = jnp.concatenate([field[1:], field[-1:]], axis=0)
    lower = jnp.concatenate([field[:1], field[:-1]], axis=0)
    return upper + lower - 2.0 * field


def shards(
    parent_field,
    parent_sppt,
    child_storm,
    child_sppt,
    wind,
    strip_dest,
    strip_row,
    strip_target,
    storm_shift,
):
    devices = lax.axis_size(("gx", "gy"))
    my_index = lax.axis_index(("gx", "gy"))
    wind_x = wind[0][:, None, None]
    wind_y = wind[1][:, None, None]
    new_parent = parent_field + (1.0 + parent_sppt.astype(jnp.float32)) * (
        halo_tendency(parent_field, wind_x, wind_y) + VERTICAL * vertical(parent_field)
    )
    levels, crows, widths = child_storm.shape
    npiece = storm_shift.shape[1]
    band_rows = crows // npiece
    nx, ny = lax.axis_size("gx"), lax.axis_size("gy")
    child = storm_rows(child_storm, storm_shift, nx, ny)
    dest_table = strip_dest.reshape(devices, -1)
    row_table = strip_row.reshape(devices, -1)
    target_table = strip_target.reshape(devices, -1)
    slots = dest_table.shape[1]
    my_dest = lax.dynamic_index_in_dim(dest_table, my_index, 0, keepdims=False)
    my_rows = lax.dynamic_index_in_dim(row_table, my_index, 0, keepdims=False)
    same_owner = my_dest[:, None] == my_dest[None, :]
    earlier = jnp.arange(slots)[None, :] < jnp.arange(slots)[:, None]
    rank = jnp.sum((same_owner & earlier).astype(jnp.int32), axis=1)
    slot_index = my_dest * CAP + rank
    send_select = jnp.arange(devices * CAP)[:, None] == slot_index[None, :]
    valid = jnp.any(send_select, axis=1)
    source = jnp.sum(jnp.where(send_select, jnp.arange(slots)[None, :], 0), axis=1)
    strip_rows = jnp.take(my_rows, source)
    per_row = parent_field.shape[2] // STRIP
    block_row = strip_rows // per_row
    block_pick = (strip_rows[:, None] % per_row == jnp.arange(per_row)[None, :]) & valid[:, None]

    def pick(state):
        rows = jnp.take(state, block_row, axis=1).reshape(levels, -1, per_row, STRIP)
        return jnp.sum(jnp.where(block_pick[None, :, :, None], rows, 0.0), axis=2)

    outgoing = jnp.stack([pick(parent_field), pick(new_parent)])
    outgoing = jnp.transpose(outgoing, (2, 0, 1, 3)) + 0.0 * child[0, 0, 0]
    incoming = lax.all_to_all(outgoing, ("gx", "gy"), split_axis=0, concat_axis=0, tiled=True)
    mine = dest_table == my_index
    rank_all = jnp.cumsum(mine.astype(jnp.int32), axis=1) - 1
    slot_ids = jnp.arange(CAP)
    hits = mine[:, None, :] & (rank_all[:, None, :] == slot_ids[None, :, None])
    chosen = jnp.sum(jnp.where(hits, target_table[:, None, :], 0), axis=2)
    target_rows = jnp.where(jnp.any(hits, axis=2), chosen, -1).reshape(-1)
    row_select = (jnp.arange(crows)[:, None] == target_rows[None, :]).astype(jnp.float32)
    coarse = jnp.einsum(
        "tq,qald->altd", row_select, incoming, precision=lax.Precision.HIGHEST
    )
    counts = jnp.sum(row_select, axis=1)
    boundary = jnp.einsum(
        "altd,de->alte",
        coarse,
        refine_table(STRIP),
        precision=lax.Precision.HIGHEST,
    )
    divisor = jnp.broadcast_to(1.0 + NUDGE * counts[:, None], (crows, widths))
    factor = 1.0 + child_sppt.astype(jnp.float32)
    edges = (child[:, 0, :], child[:, -1, :], child[:, :, 0].T, child[:, :, -1].T)
    for substep_index in range(SUBSTEPS):
        first_row, last_row, first_col, last_col = edges
        before_x = swap_edge(last_row, "gx", True)
        after_x = swap_edge(first_row, "gx", False)
        before_y = swap_edge(last_col, "gy", True)
        after_y = swap_edge(first_col, "gy", False)
        weight = (substep_index + 1) / 3.0
        child, *edges = substep(
            weight, wind, child, before_x, after_x, before_y, after_y, boundary, factor, divisor
        )
    return (new_parent, child)


def solution(mesh):
    placed = (
        P(None, "gx", "gy"),
        P("gx", "gy"),
        P(None, "gx", "gy"),
        P("gx", "gy"),
        P(),
        P(),
        P(),
        P(),
        P(),
    )
    return jax.shard_map(
        shards,
        mesh=mesh,
        in_specs=placed,
        out_specs=(P(None, "gx", "gy"), P(None, "gx", "gy")),
        check_vma=False,
    )
```

```python
import jax
import jax.numpy as jnp
from jax import lax
from jax.sharding import PartitionSpec as P
from jax.experimental import pallas as pl
from jax.experimental.pallas import tpu as pltpu
import functools

SUBSTEPS = 3
STRIP = 128
CAP = 2


KAPPA = 0.1
VERTICAL = 0.1
NUDGE = 0.5


def edge_halos(block):
    def swap(edge, axis, forward):
        count = lax.axis_size(axis)
        pairs = [(i, i + 1) for i in range(count - 1)]
        if not forward:
            pairs = [(target, source) for source, target in pairs]
        return lax.ppermute(edge, axis, pairs)

    before_x = swap(block[:, -1, :], "gx", True)
    after_x = swap(block[:, 0, :], "gx", False)
    before_y = swap(block[:, :, -1], "gy", True)
    after_y = swap(block[:, :, 0], "gy", False)
    return before_x, after_x, before_y, after_y


def halo_tendency(block, wind_x, wind_y):
    before_x, after_x, before_y, after_y = edge_halos(block)
    north = jnp.concatenate([block[:, 1:, :], after_x[:, None, :]], axis=1)
    south = jnp.concatenate([before_x[:, None, :], block[:, :-1, :]], axis=1)
    east = jnp.concatenate([block[:, :, 1:], after_y[:, :, None]], axis=2)
    west = jnp.concatenate([before_y[:, :, None], block[:, :, :-1]], axis=2)
    laplace = north + south + east + west - 4.0 * block
    return KAPPA * laplace - wind_x * (0.5 * (north - south)) - wind_y * (0.5 * (east - west))


def from_behind(value, axis, steps):
    count = lax.axis_size(axis)
    pairs = [(source, (source + steps) % count) for source in range(count)]
    return lax.ppermute(value, axis, pairs)


def storm_rows(child, storm_shift, nx, ny):
    levels, crows, widths = child.shape
    mine = lax.axis_index(("gx", "gy"))
    gathered = lax.all_to_all(child, ("gx", "gy"), 1, 1, tiled=True)
    piece = mine // (crows // storm_shift.shape[1])
    grid = gathered.reshape(levels, nx, ny, widths)
    grid = jnp.roll(grid, storm_shift[0, piece], axis=1)
    grid = jnp.roll(grid, storm_shift[1, piece], axis=2)
    return lax.all_to_all(grid.reshape(levels, crows, widths), ("gx", "gy"), 1, 1, tiled=True)


def substep_kernel(weight, wind_ref, child_ref, bx_ref, ax_ref, by_ref, ay_ref, bound_ref,
                   factor_ref, divisor_ref, out_ref, first_row_ref, last_row_ref, first_col_ref, last_col_ref):
    levels, rows, cols = child_ref.shape
    row_id = lax.broadcasted_iota(jnp.int32, (rows, cols), 0)
    col_id = lax.broadcasted_iota(jnp.int32, (rows, cols), 1)
    factor = factor_ref[...]
    divisor = divisor_ref[...]
    for l in range(levels):
        c = child_ref[l]
        north = jnp.where(row_id == rows - 1, ax_ref[l:l + 1, :], pltpu.roll(c, rows - 1, 0))
        south = jnp.where(row_id == 0, bx_ref[l:l + 1, :], pltpu.roll(c, 1, 0))
        east = jnp.where(col_id == cols - 1, ay_ref[:, l:l + 1], pltpu.roll(c, cols - 1, 1))
        west = jnp.where(col_id == 0, by_ref[:, l:l + 1], pltpu.roll(c, 1, 1))
        laplace = north + south + east + west - 4.0 * c
        tend = KAPPA * laplace - wind_ref[0, l] * (0.5 * (north - south)) - wind_ref[1, l] * (0.5 * (east - west))
        b0 = bound_ref[0, l]
        target = b0 + weight * (bound_ref[1, l] - b0)
        new = (c + factor * tend + NUDGE * target) / divisor
        out_ref[l] = new
        first_row_ref[l:l + 1, :] = new[0:1, :]
        last_row_ref[l:l + 1, :] = new[rows - 1:rows, :]
        first_col_ref[:, l:l + 1] = new[:, 0:1]
        last_col_ref[:, l:l + 1] = new[:, cols - 1:cols]


def substep(weight, wind, child, bx, ax, by, ay, bound, factor, divisor):
    levels, rows, cols = child.shape
    vmem = pl.BlockSpec(memory_space=pltpu.VMEM)
    smem = pl.BlockSpec(memory_space=pltpu.SMEM)
    f32 = jnp.float32
    return pl.pallas_call(
        functools.partial(substep_kernel, weight),
        out_shape=(
            jax.ShapeDtypeStruct((levels, rows, cols), f32),
            jax.ShapeDtypeStruct((levels, cols), f32),
            jax.ShapeDtypeStruct((levels, cols), f32),
            jax.ShapeDtypeStruct((rows, levels), f32),
            jax.ShapeDtypeStruct((rows, levels), f32),
        ),
        in_specs=[smem] + [vmem] * 8,
        out_specs=(vmem,) * 5,
        cost_estimate=pl.CostEstimate(
            flops=30 * levels * rows * cols, transcendentals=0,
            bytes_accessed=4 * (4 * levels * rows * cols + 2 * rows * cols)),
    )(wind, child, bx, ax, by, ay, bound, factor, divisor)


def swap_edge(edge, axis, forward):
    count = lax.axis_size(axis)
    pairs = [(i, i + 1) for i in range(count - 1)]
    if not forward:
        pairs = [(target, source) for source, target in pairs]
    return lax.ppermute(edge, axis, pairs)


def refine_table(strip):
    coarse = jnp.arange(strip).astype(jnp.float32)
    finer = jnp.arange(3 * strip).astype(jnp.float32)
    position = jnp.clip((finer + 0.5) / 3.0 - 0.5, 0.0, strip - 1.0)
    return jnp.maximum(0.0, 1.0 - jnp.abs(position[None, :] - coarse[:, None]))


def vertical(field):
    upper = jnp.concatenate([field[1:], field[-1:]], axis=0)
    lower = jnp.concatenate([field[:1], field[:-1]], axis=0)
    return upper + lower - 2.0 * field


def shards(
    parent_field,
    parent_sppt,
    child_storm,
    child_sppt,
    wind,
    strip_dest,
    strip_row,
    strip_target,
    storm_shift,
):
    devices = lax.axis_size(("gx", "gy"))
    my_index = lax.axis_index(("gx", "gy"))
    wind_x = wind[0][:, None, None]
    wind_y = wind[1][:, None, None]
    new_parent = parent_field + (1.0 + parent_sppt.astype(jnp.float32)) * (
        halo_tendency(parent_field, wind_x, wind_y) + VERTICAL * vertical(parent_field)
    )
    levels, crows, widths = child_storm.shape
    npiece = storm_shift.shape[1]
    band_rows = crows // npiece
    nx, ny = lax.axis_size("gx"), lax.axis_size("gy")
    child = storm_rows(child_storm, storm_shift, nx, ny)
    dest_table = strip_dest.reshape(devices, -1)
    row_table = strip_row.reshape(devices, -1)
    target_table = strip_target.reshape(devices, -1)
    slots = dest_table.shape[1]
    my_dest = lax.dynamic_index_in_dim(dest_table, my_index, 0, keepdims=False)
    my_rows = lax.dynamic_index_in_dim(row_table, my_index, 0, keepdims=False)
    same_owner = my_dest[:, None] == my_dest[None, :]
    earlier = jnp.arange(slots)[None, :] < jnp.arange(slots)[:, None]
    rank = jnp.sum((same_owner & earlier).astype(jnp.int32), axis=1)
    slot_index = my_dest * CAP + rank
    send_select = (jnp.arange(devices * CAP)[:, None] == slot_index[None, :]).astype(jnp.float32)
    both_states = jnp.stack([parent_field, new_parent]).reshape(2, levels, -1, STRIP)
    picked = jnp.take(both_states, my_rows, axis=2)
    strip_values = jnp.moveaxis(picked, 2, 0).reshape(slots, -1)
    outgoing_strips = jnp.dot(
        send_select,
        strip_values,
        precision=lax.Precision.HIGH,
        preferred_element_type=jnp.float32,
    )
    outgoing_strips = outgoing_strips + 0.0 * child[0, 0, 0]
    incoming = lax.all_to_all(
        outgoing_strips, ("gx", "gy"), split_axis=0, concat_axis=0, tiled=True
    )
    mine = dest_table == my_index
    rank_all = jnp.cumsum(mine.astype(jnp.int32), axis=1) - 1
    slot_ids = jnp.arange(CAP)
    hits = mine[:, None, :] & (rank_all[:, None, :] == slot_ids[None, :, None])
    chosen = jnp.sum(jnp.where(hits, target_table[:, None, :], 0), axis=2)
    target_rows = jnp.where(jnp.any(hits, axis=2), chosen, -1).reshape(-1)
    row_select = (jnp.arange(crows)[:, None] == target_rows[None, :]).astype(jnp.float32)
    coarse = jnp.dot(
        row_select, incoming, precision=lax.Precision.HIGH, preferred_element_type=jnp.float32
    )
    counts = jnp.sum(row_select, axis=1)
    boundary = jnp.einsum(
        "tald,de->alte",
        coarse.reshape(crows, 2, levels, STRIP),
        refine_table(STRIP),
        precision=lax.Precision.HIGH,
    )
    divisor = jnp.broadcast_to(1.0 + NUDGE * counts[:, None], (crows, widths))
    factor = 1.0 + child_sppt.astype(jnp.float32)
    edges = (child[:, 0, :], child[:, -1, :], child[:, :, 0].T, child[:, :, -1].T)
    for substep_index in range(SUBSTEPS):
        first_row, last_row, first_col, last_col = edges
        before_x = swap_edge(last_row, "gx", True)
        after_x = swap_edge(first_row, "gx", False)
        before_y = swap_edge(last_col, "gy", True)
        after_y = swap_edge(first_col, "gy", False)
        weight = (substep_index + 1) / 3.0
        child, *edges = substep(
            weight, wind, child, before_x, after_x, before_y, after_y, boundary, factor, divisor
        )
    return (new_parent, child)


def solution(mesh):
    placed = (
        P(None, "gx", "gy"),
        P("gx", "gy"),
        P(None, "gx", "gy"),
        P("gx", "gy"),
        P(),
        P(),
        P(),
        P(),
        P(),
    )
    return jax.shard_map(
        shards,
        mesh=mesh,
        in_specs=placed,
        out_specs=(P(None, "gx", "gy"), P(None, "gx", "gy")),
        check_vma=False,
    )
```

```python
import jax
import jax.numpy as jnp
from jax import lax
from jax.sharding import PartitionSpec as P
from jax.experimental import pallas as pl
from jax.experimental.pallas import tpu as pltpu
import functools

SUBSTEPS = 3
STRIP = 128
CAP = 2


KAPPA = 0.1
VERTICAL = 0.1
NUDGE = 0.5


def edge_halos(block):
    def swap(edge, axis, forward):
        count = lax.axis_size(axis)
        pairs = [(i, i + 1) for i in range(count - 1)]
        if not forward:
            pairs = [(target, source) for source, target in pairs]
        return lax.ppermute(edge, axis, pairs)

    before_x = swap(block[:, -1, :], "gx", True)
    after_x = swap(block[:, 0, :], "gx", False)
    before_y = swap(block[:, :, -1], "gy", True)
    after_y = swap(block[:, :, 0], "gy", False)
    return before_x, after_x, before_y, after_y


def halo_tendency(block, wind_x, wind_y):
    before_x, after_x, before_y, after_y = edge_halos(block)
    north = jnp.concatenate([block[:, 1:, :], after_x[:, None, :]], axis=1)
    south = jnp.concatenate([before_x[:, None, :], block[:, :-1, :]], axis=1)
    east = jnp.concatenate([block[:, :, 1:], after_y[:, :, None]], axis=2)
    west = jnp.concatenate([before_y[:, :, None], block[:, :, :-1]], axis=2)
    laplace = north + south + east + west - 4.0 * block
    return KAPPA * laplace - wind_x * (0.5 * (north - south)) - wind_y * (0.5 * (east - west))


def from_behind(value, axis, steps):
    count = lax.axis_size(axis)
    pairs = [(source, (source + steps) % count) for source in range(count)]
    return lax.ppermute(value, axis, pairs)


def storm_rows(child, storm_shift, nx, ny):
    levels, crows, widths = child.shape
    mine = lax.axis_index(("gx", "gy"))
    gathered = lax.all_to_all(child, ("gx", "gy"), 1, 1, tiled=True)
    piece = mine // (crows // storm_shift.shape[1])
    grid = gathered.reshape(levels, nx, ny, widths)
    grid = jnp.roll(grid, storm_shift[0, piece], axis=1)
    grid = jnp.roll(grid, storm_shift[1, piece], axis=2)
    return lax.all_to_all(grid.reshape(levels, crows, widths), ("gx", "gy"), 1, 1, tiled=True)


def substep_kernel(weight, wind_ref, child_ref, bx_ref, ax_ref, by_ref, ay_ref, bound_ref,
                   factor_ref, divisor_ref, out_ref, first_row_ref, last_row_ref, first_col_ref, last_col_ref):
    l = pl.program_id(0)
    _, rows, cols = child_ref.shape
    levels = bx_ref.shape[0]
    row_id = lax.broadcasted_iota(jnp.int32, (rows, cols), 0)
    col_id = lax.broadcasted_iota(jnp.int32, (rows, cols), 1)
    level_id = lax.broadcasted_iota(jnp.int32, (rows, levels), 1)
    by_col = jnp.sum(jnp.where(level_id == l, by_ref[...].T, 0.0), axis=1, keepdims=True)
    ay_col = jnp.sum(jnp.where(level_id == l, ay_ref[...].T, 0.0), axis=1, keepdims=True)
    c = child_ref[0]
    north = jnp.where(row_id == rows - 1, ax_ref[pl.ds(l, 1), :], pltpu.roll(c, rows - 1, 0))
    south = jnp.where(row_id == 0, bx_ref[pl.ds(l, 1), :], pltpu.roll(c, 1, 0))
    east = jnp.where(col_id == cols - 1, ay_col, pltpu.roll(c, cols - 1, 1))
    west = jnp.where(col_id == 0, by_col, pltpu.roll(c, 1, 1))
    laplace = north + south + east + west - 4.0 * c
    tend = KAPPA * laplace - wind_ref[0, l] * (0.5 * (north - south)) - wind_ref[1, l] * (0.5 * (east - west))
    b0 = bound_ref[0, 0]
    target = b0 + weight * (bound_ref[1, 0] - b0)
    new = (c + factor_ref[...] * tend + NUDGE * target) / divisor_ref[...]
    out_ref[0] = new
    first_row_ref[pl.ds(l, 1), :] = new[0:1, :]
    last_row_ref[pl.ds(l, 1), :] = new[rows - 1:rows, :]
    first_col_ref[pl.ds(l, 1), :] = new[:, 0:rows].T[0:1, :]
    last_col_ref[pl.ds(l, 1), :] = new[:, cols - rows:cols].T[rows - 1:rows, :]


def substep(weight, wind, child, bx, ax, by, ay, bound, factor, divisor):
    levels, rows, cols = child.shape
    f32 = jnp.float32
    whole = lambda shape: pl.BlockSpec(shape, lambda l: (0,) * len(shape))
    level_block = pl.BlockSpec((1, rows, cols), lambda l: (l, 0, 0))
    return pl.pallas_call(
        functools.partial(substep_kernel, weight),
        grid=(levels,),
        out_shape=(
            jax.ShapeDtypeStruct((levels, rows, cols), f32),
            jax.ShapeDtypeStruct((levels, cols), f32),
            jax.ShapeDtypeStruct((levels, cols), f32),
            jax.ShapeDtypeStruct((levels, rows), f32),
            jax.ShapeDtypeStruct((levels, rows), f32),
        ),
        in_specs=[
            pl.BlockSpec(memory_space=pltpu.SMEM),
            level_block,
            whole((levels, cols)),
            whole((levels, cols)),
            whole((levels, rows)),
            whole((levels, rows)),
            pl.BlockSpec((2, 1, rows, cols), lambda l: (0, l, 0, 0)),
            whole((rows, cols)),
            whole((rows, cols)),
        ],
        out_specs=(
            level_block,
            whole((levels, cols)),
            whole((levels, cols)),
            whole((levels, rows)),
            whole((levels, rows)),
        ),
        compiler_params=pltpu.CompilerParams(dimension_semantics=("arbitrary",)),
        cost_estimate=pl.CostEstimate(
            flops=30 * levels * rows * cols, transcendentals=0,
            bytes_accessed=4 * (4 * levels * rows * cols + 2 * rows * cols)),
    )(wind, child, bx, ax, by, ay, bound, factor, divisor)


def swap_edge(edge, axis, forward):
    count = lax.axis_size(axis)
    pairs = [(i, i + 1) for i in range(count - 1)]
    if not forward:
        pairs = [(target, source) for source, target in pairs]
    return lax.ppermute(edge, axis, pairs)


def refine_table(strip):
    coarse = jnp.arange(strip).astype(jnp.float32)
    finer = jnp.arange(3 * strip).astype(jnp.float32)
    position = jnp.clip((finer + 0.5) / 3.0 - 0.5, 0.0, strip - 1.0)
    return jnp.maximum(0.0, 1.0 - jnp.abs(position[None, :] - coarse[:, None]))


def vertical(field):
    upper = jnp.concatenate([field[1:], field[-1:]], axis=0)
    lower = jnp.concatenate([field[:1], field[:-1]], axis=0)
    return upper + lower - 2.0 * field


def shards(
    parent_field,
    parent_sppt,
    child_storm,
    child_sppt,
    wind,
    strip_dest,
    strip_row,
    strip_target,
    storm_shift,
):
    devices = lax.axis_size(("gx", "gy"))
    my_index = lax.axis_index(("gx", "gy"))
    wind_x = wind[0][:, None, None]
    wind_y = wind[1][:, None, None]
    new_parent = parent_field + (1.0 + parent_sppt.astype(jnp.float32)) * (
        halo_tendency(parent_field, wind_x, wind_y) + VERTICAL * vertical(parent_field)
    )
    levels, crows, widths = child_storm.shape
    npiece = storm_shift.shape[1]
    band_rows = crows // npiece
    nx, ny = lax.axis_size("gx"), lax.axis_size("gy")
    child = storm_rows(child_storm, storm_shift, nx, ny)
    dest_table = strip_dest.reshape(devices, -1)
    row_table = strip_row.reshape(devices, -1)
    target_table = strip_target.reshape(devices, -1)
    slots = dest_table.shape[1]
    my_dest = lax.dynamic_index_in_dim(dest_table, my_index, 0, keepdims=False)
    my_rows = lax.dynamic_index_in_dim(row_table, my_index, 0, keepdims=False)
    same_owner = my_dest[:, None] == my_dest[None, :]
    earlier = jnp.arange(slots)[None, :] < jnp.arange(slots)[:, None]
    rank = jnp.sum((same_owner & earlier).astype(jnp.int32), axis=1)
    slot_index = my_dest * CAP + rank
    send_select = (jnp.arange(devices * CAP)[:, None] == slot_index[None, :]).astype(jnp.float32)
    both_states = jnp.stack([parent_field, new_parent]).reshape(2, levels, -1, STRIP)
    picked = jnp.take(both_states, my_rows, axis=2)
    strip_values = jnp.moveaxis(picked, 2, 0).reshape(slots, -1)
    outgoing_strips = jnp.dot(
        send_select,
        strip_values,
        precision=lax.Precision.HIGH,
        preferred_element_type=jnp.float32,
    )
    outgoing_strips = outgoing_strips + 0.0 * child[0, 0, 0]
    incoming = lax.all_to_all(
        outgoing_strips, ("gx", "gy"), split_axis=0, concat_axis=0, tiled=True
    )
    mine = dest_table == my_index
    rank_all = jnp.cumsum(mine.astype(jnp.int32), axis=1) - 1
    slot_ids = jnp.arange(CAP)
    hits = mine[:, None, :] & (rank_all[:, None, :] == slot_ids[None, :, None])
    chosen = jnp.sum(jnp.where(hits, target_table[:, None, :], 0), axis=2)
    target_rows = jnp.where(jnp.any(hits, axis=2), chosen, -1).reshape(-1)
    row_select = (jnp.arange(crows)[:, None] == target_rows[None, :]).astype(jnp.float32)
    coarse = jnp.dot(
        row_select, incoming, precision=lax.Precision.HIGH, preferred_element_type=jnp.float32
    )
    counts = jnp.sum(row_select, axis=1)
    boundary = jnp.einsum(
        "tald,de->alte",
        coarse.reshape(crows, 2, levels, STRIP),
        refine_table(STRIP),
        precision=lax.Precision.HIGH,
    )
    divisor = jnp.broadcast_to(1.0 + NUDGE * counts[:, None], (crows, widths))
    factor = 1.0 + child_sppt.astype(jnp.float32)
    edges = (child[:, 0, :], child[:, -1, :], child[:, :, 0], child[:, :, -1])
    for substep_index in range(SUBSTEPS):
        first_row, last_row, first_col, last_col = edges
        before_x = swap_edge(last_row, "gx", True)
        after_x = swap_edge(first_row, "gx", False)
        before_y = swap_edge(last_col, "gy", True)
        after_y = swap_edge(first_col, "gy", False)
        weight = (substep_index + 1) / 3.0
        child, *edges = substep(
            weight, wind, child, before_x, after_x, before_y, after_y, boundary, factor, divisor
        )
    return (new_parent, child)


def solution(mesh):
    placed = (
        P(None, "gx", "gy"),
        P("gx", "gy"),
        P(None, "gx", "gy"),
        P("gx", "gy"),
        P(),
        P(),
        P(),
        P(),
        P(),
    )
    return jax.shard_map(
        shards,
        mesh=mesh,
        in_specs=placed,
        out_specs=(P(None, "gx", "gy"), P(None, "gx", "gy")),
        check_vma=False,
    )
```

```python
import jax
import jax.numpy as jnp
from jax import lax
from jax.sharding import PartitionSpec as P
from jax.experimental import pallas as pl
from jax.experimental.pallas import tpu as pltpu
import functools

SUBSTEPS = 3
STRIP = 128
CAP = 2


KAPPA = 0.1
VERTICAL = 0.1
NUDGE = 0.5


def edge_halos(block):
    def swap(edge, axis, forward):
        count = lax.axis_size(axis)
        pairs = [(i, i + 1) for i in range(count - 1)]
        if not forward:
            pairs = [(target, source) for source, target in pairs]
        return lax.ppermute(edge, axis, pairs)

    before_x = swap(block[:, -1, :], "gx", True)
    after_x = swap(block[:, 0, :], "gx", False)
    before_y = swap(block[:, :, -1], "gy", True)
    after_y = swap(block[:, :, 0], "gy", False)
    return before_x, after_x, before_y, after_y


def halo_tendency(block, wind_x, wind_y):
    before_x, after_x, before_y, after_y = edge_halos(block)
    north = jnp.concatenate([block[:, 1:, :], after_x[:, None, :]], axis=1)
    south = jnp.concatenate([before_x[:, None, :], block[:, :-1, :]], axis=1)
    east = jnp.concatenate([block[:, :, 1:], after_y[:, :, None]], axis=2)
    west = jnp.concatenate([before_y[:, :, None], block[:, :, :-1]], axis=2)
    laplace = north + south + east + west - 4.0 * block
    return KAPPA * laplace - wind_x * (0.5 * (north - south)) - wind_y * (0.5 * (east - west))


def from_behind(value, axis, steps):
    count = lax.axis_size(axis)
    pairs = [(source, (source + steps) % count) for source in range(count)]
    return lax.ppermute(value, axis, pairs)


def storm_rows(child, storm_shift, nx, ny):
    levels, crows, widths = child.shape
    mine = lax.axis_index(("gx", "gy"))
    gathered = lax.all_to_all(child, ("gx", "gy"), 1, 1, tiled=True)
    piece = mine // (crows // storm_shift.shape[1])
    grid = gathered.reshape(levels, nx, ny, widths)
    grid = jnp.roll(grid, storm_shift[0, piece], axis=1)
    grid = jnp.roll(grid, storm_shift[1, piece], axis=2)
    return lax.all_to_all(grid.reshape(levels, crows, widths), ("gx", "gy"), 1, 1, tiled=True)


def substep_kernel(weight, wind_ref, child_ref, bx_ref, ax_ref, by_ref, ay_ref, bound_ref,
                   factor_ref, divisor_ref, out_ref, first_row_ref, last_row_ref, first_col_ref, last_col_ref):
    levels, rows, cols = child_ref.shape
    row_id = lax.broadcasted_iota(jnp.int32, (rows, cols), 0)
    col_id = lax.broadcasted_iota(jnp.int32, (rows, cols), 1)
    factor = factor_ref[...]
    divisor = divisor_ref[...]
    for l in range(levels):
        c = child_ref[l]
        north = jnp.where(row_id == rows - 1, ax_ref[l:l + 1, :], pltpu.roll(c, rows - 1, 0))
        south = jnp.where(row_id == 0, bx_ref[l:l + 1, :], pltpu.roll(c, 1, 0))
        east = jnp.where(col_id == cols - 1, ay_ref[:, l:l + 1], pltpu.roll(c, cols - 1, 1))
        west = jnp.where(col_id == 0, by_ref[:, l:l + 1], pltpu.roll(c, 1, 1))
        laplace = north + south + east + west - 4.0 * c
        tend = KAPPA * laplace - wind_ref[0, l] * (0.5 * (north - south)) - wind_ref[1, l] * (0.5 * (east - west))
        b0 = bound_ref[0, l]
        target = b0 + weight * (bound_ref[1, l] - b0)
        new = (c + factor * tend + NUDGE * target) / divisor
        out_ref[l] = new
        first_row_ref[l:l + 1, :] = new[0:1, :]
        last_row_ref[l:l + 1, :] = new[rows - 1:rows, :]
        first_col_ref[:, l:l + 1] = new[:, 0:1]
        last_col_ref[:, l:l + 1] = new[:, cols - 1:cols]


def substep(weight, wind, child, bx, ax, by, ay, bound, factor, divisor):
    levels, rows, cols = child.shape
    vmem = pl.BlockSpec(memory_space=pltpu.VMEM)
    smem = pl.BlockSpec(memory_space=pltpu.SMEM)
    f32 = jnp.float32
    return pl.pallas_call(
        functools.partial(substep_kernel, weight),
        out_shape=(
            jax.ShapeDtypeStruct((levels, rows, cols), f32),
            jax.ShapeDtypeStruct((levels, cols), f32),
            jax.ShapeDtypeStruct((levels, cols), f32),
            jax.ShapeDtypeStruct((rows, levels), f32),
            jax.ShapeDtypeStruct((rows, levels), f32),
        ),
        in_specs=[smem] + [vmem] * 8,
        out_specs=(vmem,) * 5,
        cost_estimate=pl.CostEstimate(
            flops=30 * levels * rows * cols, transcendentals=0,
            bytes_accessed=4 * (4 * levels * rows * cols + 2 * rows * cols)),
    )(wind, child, bx, ax, by, ay, bound, factor, divisor)


def swap_edge(edge, axis, forward):
    count = lax.axis_size(axis)
    pairs = [(i, i + 1) for i in range(count - 1)]
    if not forward:
        pairs = [(target, source) for source, target in pairs]
    return lax.ppermute(edge, axis, pairs)


def refine_table(strip):
    coarse = jnp.arange(strip).astype(jnp.float32)
    finer = jnp.arange(3 * strip).astype(jnp.float32)
    position = jnp.clip((finer + 0.5) / 3.0 - 0.5, 0.0, strip - 1.0)
    return jnp.maximum(0.0, 1.0 - jnp.abs(position[None, :] - coarse[:, None]))


def vertical(field):
    upper = jnp.concatenate([field[1:], field[-1:]], axis=0)
    lower = jnp.concatenate([field[:1], field[:-1]], axis=0)
    return upper + lower - 2.0 * field


def shards(
    parent_field,
    parent_sppt,
    child_storm,
    child_sppt,
    wind,
    strip_dest,
    strip_row,
    strip_target,
    storm_shift,
):
    devices = lax.axis_size(("gx", "gy"))
    my_index = lax.axis_index(("gx", "gy"))
    wind_x = wind[0][:, None, None]
    wind_y = wind[1][:, None, None]
    new_parent = parent_field + (1.0 + parent_sppt.astype(jnp.float32)) * (
        halo_tendency(parent_field, wind_x, wind_y) + VERTICAL * vertical(parent_field)
    )
    levels, crows, widths = child_storm.shape
    npiece = storm_shift.shape[1]
    band_rows = crows // npiece
    nx, ny = lax.axis_size("gx"), lax.axis_size("gy")
    child = storm_rows(child_storm, storm_shift, nx, ny)
    dest_table = strip_dest.reshape(devices, -1)
    row_table = strip_row.reshape(devices, -1)
    target_table = strip_target.reshape(devices, -1)
    slots = dest_table.shape[1]
    my_dest = lax.dynamic_index_in_dim(dest_table, my_index, 0, keepdims=False)
    my_rows = lax.dynamic_index_in_dim(row_table, my_index, 0, keepdims=False)
    same_owner = my_dest[:, None] == my_dest[None, :]
    earlier = jnp.arange(slots)[None, :] < jnp.arange(slots)[:, None]
    rank = jnp.sum((same_owner & earlier).astype(jnp.int32), axis=1)
    slot_index = my_dest * CAP + rank
    send_select = (jnp.arange(devices * CAP)[:, None] == slot_index[None, :]).astype(jnp.float32)
    both_states = jnp.stack([parent_field, new_parent]).reshape(2, levels, -1, STRIP)
    picked = jnp.take(both_states, my_rows, axis=2)
    strip_values = jnp.moveaxis(picked, 2, 0).reshape(slots, -1)
    outgoing_strips = jnp.einsum(
        "dsj,jk->dsk",
        send_select.reshape(devices, CAP, slots),
        strip_values,
        precision=lax.Precision.HIGH,
    )
    outgoing_strips = outgoing_strips + 0.0 * child[0, 0, 0]
    incoming = lax.all_to_all(
        outgoing_strips, ("gx", "gy"), split_axis=0, concat_axis=0, tiled=True
    )
    mine = dest_table == my_index
    rank_all = jnp.cumsum(mine.astype(jnp.int32), axis=1) - 1
    slot_ids = jnp.arange(CAP)
    hits = mine[:, None, :] & (rank_all[:, None, :] == slot_ids[None, :, None])
    chosen = jnp.sum(jnp.where(hits, target_table[:, None, :], 0), axis=2)
    target_rows = jnp.where(jnp.any(hits, axis=2), chosen, -1).reshape(-1)
    row_select = (jnp.arange(crows)[:, None] == target_rows[None, :]).astype(jnp.float32)
    coarse = jnp.einsum(
        "tqs,qsk->tk",
        row_select.reshape(crows, devices, CAP),
        incoming,
        precision=lax.Precision.HIGH,
    )
    counts = jnp.sum(row_select, axis=1)
    boundary = jnp.einsum(
        "tald,de->alte",
        coarse.reshape(crows, 2, levels, STRIP),
        refine_table(STRIP),
        precision=lax.Precision.HIGH,
    )
    divisor = jnp.broadcast_to(1.0 + NUDGE * counts[:, None], (crows, widths))
    factor = 1.0 + child_sppt.astype(jnp.float32)
    edges = (child[:, 0, :], child[:, -1, :], child[:, :, 0].T, child[:, :, -1].T)
    for substep_index in range(SUBSTEPS):
        first_row, last_row, first_col, last_col = edges
        before_x = swap_edge(last_row, "gx", True)
        after_x = swap_edge(first_row, "gx", False)
        before_y = swap_edge(last_col, "gy", True)
        after_y = swap_edge(first_col, "gy", False)
        weight = (substep_index + 1) / 3.0
        child, *edges = substep(
            weight, wind, child, before_x, after_x, before_y, after_y, boundary, factor, divisor
        )
    return (new_parent, child)


def solution(mesh):
    placed = (
        P(None, "gx", "gy"),
        P("gx", "gy"),
        P(None, "gx", "gy"),
        P("gx", "gy"),
        P(),
        P(),
        P(),
        P(),
        P(),
    )
    return jax.shard_map(
        shards,
        mesh=mesh,
        in_specs=placed,
        out_specs=(P(None, "gx", "gy"), P(None, "gx", "gy")),
        check_vma=False,
    )
```

```python
import jax
import jax.numpy as jnp
from jax import lax
from jax.sharding import PartitionSpec as P
from jax.experimental import pallas as pl
from jax.experimental.pallas import tpu as pltpu
import functools

SUBSTEPS = 3
STRIP = 128
CAP = 2


KAPPA = 0.1
VERTICAL = 0.1
NUDGE = 0.5


def edge_halos(block):
    def swap(edge, axis, forward):
        count = lax.axis_size(axis)
        pairs = [(i, i + 1) for i in range(count - 1)]
        if not forward:
            pairs = [(target, source) for source, target in pairs]
        return lax.ppermute(edge, axis, pairs)

    before_x = swap(block[:, -1, :], "gx", True)
    after_x = swap(block[:, 0, :], "gx", False)
    before_y = swap(block[:, :, -1], "gy", True)
    after_y = swap(block[:, :, 0], "gy", False)
    return before_x, after_x, before_y, after_y


def halo_tendency(block, wind_x, wind_y, halos):
    before_x, after_x, before_y, after_y = halos
    north = jnp.concatenate([block[:, 1:, :], after_x[:, None, :]], axis=1)
    south = jnp.concatenate([before_x[:, None, :], block[:, :-1, :]], axis=1)
    east = jnp.concatenate([block[:, :, 1:], after_y[:, :, None]], axis=2)
    west = jnp.concatenate([before_y[:, :, None], block[:, :, :-1]], axis=2)
    laplace = north + south + east + west - 4.0 * block
    return KAPPA * laplace - wind_x * (0.5 * (north - south)) - wind_y * (0.5 * (east - west))


def storm_rows(child, storm_shift, nx, ny):
    levels, crows, widths = child.shape
    mine = lax.axis_index(("gx", "gy"))
    gathered = lax.all_to_all(child, ("gx", "gy"), 1, 1, tiled=True)
    piece = mine // (crows // storm_shift.shape[1])
    grid = gathered.reshape(levels, nx, ny, widths)
    grid = jnp.roll(grid, storm_shift[0, piece], axis=1)
    grid = jnp.roll(grid, storm_shift[1, piece], axis=2)
    return lax.all_to_all(grid.reshape(levels, crows, widths), ("gx", "gy"), 1, 1, tiled=True)


def substep_kernel(weight, wind_ref, child_ref, bx_ref, ax_ref, by_ref, ay_ref, bound_ref,
                   factor_ref, divisor_ref, out_ref, first_row_ref, last_row_ref, first_col_ref, last_col_ref):
    levels, rows, cols = child_ref.shape
    row_id = lax.broadcasted_iota(jnp.int32, (rows, cols), 0)
    col_id = lax.broadcasted_iota(jnp.int32, (rows, cols), 1)
    factor = factor_ref[...]
    divisor = divisor_ref[...]
    for l in range(levels):
        c = child_ref[l]
        north = jnp.where(row_id == rows - 1, ax_ref[l:l + 1, :], pltpu.roll(c, rows - 1, 0))
        south = jnp.where(row_id == 0, bx_ref[l:l + 1, :], pltpu.roll(c, 1, 0))
        east = jnp.where(col_id == cols - 1, ay_ref[:, l:l + 1], pltpu.roll(c, cols - 1, 1))
        west = jnp.where(col_id == 0, by_ref[:, l:l + 1], pltpu.roll(c, 1, 1))
        laplace = north + south + east + west - 4.0 * c
        tend = KAPPA * laplace - wind_ref[0, l] * (0.5 * (north - south)) - wind_ref[1, l] * (0.5 * (east - west))
        b0 = bound_ref[0, l]
        target = b0 + weight * (bound_ref[1, l] - b0)
        new = (c + factor * tend + NUDGE * target) / divisor
        out_ref[l] = new
        first_row_ref[l:l + 1, :] = new[0:1, :]
        last_row_ref[l:l + 1, :] = new[rows - 1:rows, :]
        first_col_ref[:, l:l + 1] = new[:, 0:1]
        last_col_ref[:, l:l + 1] = new[:, cols - 1:cols]


def substep(weight, wind, child, bx, ax, by, ay, bound, factor, divisor):
    levels, rows, cols = child.shape
    vmem = pl.BlockSpec(memory_space=pltpu.VMEM)
    smem = pl.BlockSpec(memory_space=pltpu.SMEM)
    f32 = jnp.float32
    return pl.pallas_call(
        functools.partial(substep_kernel, weight),
        out_shape=(
            jax.ShapeDtypeStruct((levels, rows, cols), f32),
            jax.ShapeDtypeStruct((levels, cols), f32),
            jax.ShapeDtypeStruct((levels, cols), f32),
            jax.ShapeDtypeStruct((rows, levels), f32),
            jax.ShapeDtypeStruct((rows, levels), f32),
        ),
        in_specs=[smem] + [vmem] * 8,
        out_specs=(vmem,) * 5,
        cost_estimate=pl.CostEstimate(
            flops=30 * levels * rows * cols, transcendentals=0,
            bytes_accessed=4 * (4 * levels * rows * cols + 2 * rows * cols)),
    )(wind, child, bx, ax, by, ay, bound, factor, divisor)


def swap_edge(edge, axis, forward):
    count = lax.axis_size(axis)
    pairs = [(i, i + 1) for i in range(count - 1)]
    if not forward:
        pairs = [(target, source) for source, target in pairs]
    return lax.ppermute(edge, axis, pairs)


def refine_table(strip):
    coarse = jnp.arange(strip).astype(jnp.float32)
    finer = jnp.arange(3 * strip).astype(jnp.float32)
    position = jnp.clip((finer + 0.5) / 3.0 - 0.5, 0.0, strip - 1.0)
    return jnp.maximum(0.0, 1.0 - jnp.abs(position[None, :] - coarse[:, None]))


def vertical(field):
    upper = jnp.concatenate([field[1:], field[-1:]], axis=0)
    lower = jnp.concatenate([field[:1], field[:-1]], axis=0)
    return upper + lower - 2.0 * field


def shards(
    parent_field,
    parent_sppt,
    child_storm,
    child_sppt,
    wind,
    strip_dest,
    strip_row,
    strip_target,
    storm_shift,
):
    devices = lax.axis_size(("gx", "gy"))
    my_index = lax.axis_index(("gx", "gy"))
    wind_x = wind[0][:, None, None]
    wind_y = wind[1][:, None, None]
    parent_halos = edge_halos(parent_field)
    new_parent = parent_field + (1.0 + parent_sppt.astype(jnp.float32)) * (
        halo_tendency(parent_field, wind_x, wind_y, parent_halos) + VERTICAL * vertical(parent_field)
    )
    levels, crows, widths = child_storm.shape
    nx, ny = lax.axis_size("gx"), lax.axis_size("gy")
    child = storm_rows(child_storm, storm_shift, nx, ny)
    dest_table = strip_dest.reshape(devices, -1)
    row_table = strip_row.reshape(devices, -1)
    target_table = strip_target.reshape(devices, -1)
    slots = dest_table.shape[1]
    my_dest = lax.dynamic_index_in_dim(dest_table, my_index, 0, keepdims=False)
    my_rows = lax.dynamic_index_in_dim(row_table, my_index, 0, keepdims=False)
    same_owner = my_dest[:, None] == my_dest[None, :]
    earlier = jnp.arange(slots)[None, :] < jnp.arange(slots)[:, None]
    rank = jnp.sum((same_owner & earlier).astype(jnp.int32), axis=1)
    slot_index = my_dest * CAP + rank
    send_select = (jnp.arange(devices * CAP)[:, None] == slot_index[None, :]).astype(jnp.float32)
    both_states = jnp.stack([parent_field, new_parent]).reshape(2, levels, -1, STRIP)
    picked = jnp.take(both_states, my_rows, axis=2)
    strip_values = jnp.moveaxis(picked, 2, 0).reshape(slots, -1)
    outgoing_strips = jnp.einsum(
        "dsj,jk->dsk",
        send_select.reshape(devices, CAP, slots),
        strip_values,
        precision=lax.Precision.HIGH,
    )
    outgoing_strips = outgoing_strips + 0.0 * child[0, 0, 0]
    incoming = lax.all_to_all(
        outgoing_strips, ("gx", "gy"), split_axis=0, concat_axis=0, tiled=True
    )
    mine = dest_table == my_index
    rank_all = jnp.cumsum(mine.astype(jnp.int32), axis=1) - 1
    slot_ids = jnp.arange(CAP)
    hits = mine[:, None, :] & (rank_all[:, None, :] == slot_ids[None, :, None])
    chosen = jnp.sum(jnp.where(hits, target_table[:, None, :], 0), axis=2)
    target_rows = jnp.where(jnp.any(hits, axis=2), chosen, -1).reshape(-1)
    row_select = (jnp.arange(crows)[:, None] == target_rows[None, :]).astype(jnp.float32)
    coarse = jnp.einsum(
        "tqs,qsk->tk",
        row_select.reshape(crows, devices, CAP),
        incoming,
        precision=lax.Precision.HIGH,
    )
    counts = jnp.sum(row_select, axis=1)
    boundary = jnp.einsum(
        "tald,de->alte",
        coarse.reshape(crows, 2, levels, STRIP),
        refine_table(STRIP),
        precision=lax.Precision.HIGH,
    )
    divisor = jnp.broadcast_to(1.0 + NUDGE * counts[:, None], (crows, widths))
    factor = 1.0 + child_sppt.astype(jnp.float32)
    edges = (child[:, 0, :], child[:, -1, :], child[:, :, 0].T, child[:, :, -1].T)
    for substep_index in range(SUBSTEPS):
        first_row, last_row, first_col, last_col = edges
        before_x = swap_edge(last_row, "gx", True)
        after_x = swap_edge(first_row, "gx", False)
        before_y = swap_edge(last_col, "gy", True)
        after_y = swap_edge(first_col, "gy", False)
        weight = (substep_index + 1) / 3.0
        child, *edges = substep(
            weight, wind, child, before_x, after_x, before_y, after_y, boundary, factor, divisor
        )
    return (new_parent, child)


def solution(mesh):
    placed = (
        P(None, "gx", "gy"),
        P("gx", "gy"),
        P(None, "gx", "gy"),
        P("gx", "gy"),
        P(),
        P(),
        P(),
        P(),
        P(),
    )

    return jax.shard_map(
        shards,
        mesh=mesh,
        in_specs=placed,
        out_specs=(P(None, "gx", "gy"), P(None, "gx", "gy")),
        check_vma=False,
    )
```

```python
import jax
import jax.numpy as jnp
from jax import lax
from jax.sharding import PartitionSpec as P
from jax.experimental import pallas as pl
from jax.experimental.pallas import tpu as pltpu
import functools

SUBSTEPS = 3
STRIP = 128
CAP = 2


KAPPA = 0.1
VERTICAL = 0.1
NUDGE = 0.5


def edge_halos(block):
    def swap(edge, axis, forward):
        count = lax.axis_size(axis)
        pairs = [(i, i + 1) for i in range(count - 1)]
        if not forward:
            pairs = [(target, source) for source, target in pairs]
        return lax.ppermute(edge, axis, pairs)

    before_x = swap(block[:, -1, :], "gx", True)
    after_x = swap(block[:, 0, :], "gx", False)
    before_y = swap(block[:, :, -1], "gy", True)
    after_y = swap(block[:, :, 0], "gy", False)
    return before_x, after_x, before_y, after_y


def halo_tendency(block, wind_x, wind_y, halos):
    before_x, after_x, before_y, after_y = halos
    north = jnp.concatenate([block[:, 1:, :], after_x[:, None, :]], axis=1)
    south = jnp.concatenate([before_x[:, None, :], block[:, :-1, :]], axis=1)
    east = jnp.concatenate([block[:, :, 1:], after_y[:, :, None]], axis=2)
    west = jnp.concatenate([before_y[:, :, None], block[:, :, :-1]], axis=2)
    laplace = north + south + east + west - 4.0 * block
    return KAPPA * laplace - wind_x * (0.5 * (north - south)) - wind_y * (0.5 * (east - west))


def storm_rows(child, storm_shift, nx, ny):
    levels, crows, widths = child.shape
    devices = nx * ny
    per_level = devices // levels
    piece_rows = crows // per_level
    mine = lax.axis_index(("gx", "gy"))
    pieces = child.reshape(devices, piece_rows, widths)
    gathered = lax.all_to_all(pieces, ("gx", "gy"), 0, 0, tiled=True)
    piece = (mine % per_level) * piece_rows // (crows // storm_shift.shape[1])
    grid = gathered.reshape(nx, ny, piece_rows, widths)
    grid = jnp.roll(grid, storm_shift[0, piece], axis=0)
    grid = jnp.roll(grid, storm_shift[1, piece], axis=1)
    back = lax.all_to_all(grid.reshape(devices, piece_rows, widths), ("gx", "gy"), 0, 0, tiled=True)
    return back.reshape(levels, crows, widths)


def substep_kernel(weight, wind_ref, child_ref, bx_ref, ax_ref, by_ref, ay_ref, bound_ref,
                   factor_ref, divisor_ref, out_ref, first_row_ref, last_row_ref, first_col_ref, last_col_ref):
    levels, rows, cols = child_ref.shape
    row_id = lax.broadcasted_iota(jnp.int32, (rows, cols), 0)
    col_id = lax.broadcasted_iota(jnp.int32, (rows, cols), 1)
    factor = factor_ref[...]
    divisor = divisor_ref[...]
    for l in range(levels):
        c = child_ref[l]
        north = jnp.where(row_id == rows - 1, ax_ref[l:l + 1, :], pltpu.roll(c, rows - 1, 0))
        south = jnp.where(row_id == 0, bx_ref[l:l + 1, :], pltpu.roll(c, 1, 0))
        east = jnp.where(col_id == cols - 1, ay_ref[:, l:l + 1], pltpu.roll(c, cols - 1, 1))
        west = jnp.where(col_id == 0, by_ref[:, l:l + 1], pltpu.roll(c, 1, 1))
        laplace = north + south + east + west - 4.0 * c
        tend = KAPPA * laplace - wind_ref[0, l] * (0.5 * (north - south)) - wind_ref[1, l] * (0.5 * (east - west))
        b0 = bound_ref[0, l]
        target = b0 + weight * (bound_ref[1, l] - b0)
        new = (c + factor * tend + NUDGE * target) / divisor
        out_ref[l] = new
        first_row_ref[l:l + 1, :] = new[0:1, :]
        last_row_ref[l:l + 1, :] = new[rows - 1:rows, :]
        first_col_ref[:, l:l + 1] = new[:, 0:1]
        last_col_ref[:, l:l + 1] = new[:, cols - 1:cols]


def substep(weight, wind, child, bx, ax, by, ay, bound, factor, divisor):
    levels, rows, cols = child.shape
    vmem = pl.BlockSpec(memory_space=pltpu.VMEM)
    smem = pl.BlockSpec(memory_space=pltpu.SMEM)
    f32 = jnp.float32
    return pl.pallas_call(
        functools.partial(substep_kernel, weight),
        out_shape=(
            jax.ShapeDtypeStruct((levels, rows, cols), f32),
            jax.ShapeDtypeStruct((levels, cols), f32),
            jax.ShapeDtypeStruct((levels, cols), f32),
            jax.ShapeDtypeStruct((rows, levels), f32),
            jax.ShapeDtypeStruct((rows, levels), f32),
        ),
        in_specs=[smem] + [vmem] * 8,
        out_specs=(vmem,) * 5,
        cost_estimate=pl.CostEstimate(
            flops=30 * levels * rows * cols, transcendentals=0,
            bytes_accessed=4 * (4 * levels * rows * cols + 2 * rows * cols)),
    )(wind, child, bx, ax, by, ay, bound, factor, divisor)


def swap_edge(edge, axis, forward):
    count = lax.axis_size(axis)
    pairs = [(i, i + 1) for i in range(count - 1)]
    if not forward:
        pairs = [(target, source) for source, target in pairs]
    return lax.ppermute(edge, axis, pairs)


def refine_table(strip):
    coarse = jnp.arange(strip).astype(jnp.float32)
    finer = jnp.arange(3 * strip).astype(jnp.float32)
    position = jnp.clip((finer + 0.5) / 3.0 - 0.5, 0.0, strip - 1.0)
    return jnp.maximum(0.0, 1.0 - jnp.abs(position[None, :] - coarse[:, None]))


def vertical(field):
    upper = jnp.concatenate([field[1:], field[-1:]], axis=0)
    lower = jnp.concatenate([field[:1], field[:-1]], axis=0)
    return upper + lower - 2.0 * field


def shards(
    parent_field,
    parent_sppt,
    child_storm,
    child_sppt,
    wind,
    strip_dest,
    strip_row,
    strip_target,
    storm_shift,
):
    devices = lax.axis_size(("gx", "gy"))
    my_index = lax.axis_index(("gx", "gy"))
    wind_x = wind[0][:, None, None]
    wind_y = wind[1][:, None, None]
    parent_halos = edge_halos(parent_field)
    new_parent = parent_field + (1.0 + parent_sppt.astype(jnp.float32)) * (
        halo_tendency(parent_field, wind_x, wind_y, parent_halos) + VERTICAL * vertical(parent_field)
    )
    levels, crows, widths = child_storm.shape
    nx, ny = lax.axis_size("gx"), lax.axis_size("gy")
    child = storm_rows(child_storm, storm_shift, nx, ny)
    dest_table = strip_dest.reshape(devices, -1)
    row_table = strip_row.reshape(devices, -1)
    target_table = strip_target.reshape(devices, -1)
    slots = dest_table.shape[1]
    my_dest = lax.dynamic_index_in_dim(dest_table, my_index, 0, keepdims=False)
    my_rows = lax.dynamic_index_in_dim(row_table, my_index, 0, keepdims=False)
    same_owner = my_dest[:, None] == my_dest[None, :]
    earlier = jnp.arange(slots)[None, :] < jnp.arange(slots)[:, None]
    rank = jnp.sum((same_owner & earlier).astype(jnp.int32), axis=1)
    slot_index = my_dest * CAP + rank
    send_select = (jnp.arange(devices * CAP)[:, None] == slot_index[None, :]).astype(jnp.float32)
    both_states = jnp.stack([parent_field, new_parent]).reshape(2, levels, -1, STRIP)
    picked = jnp.take(both_states, my_rows, axis=2)
    strip_values = jnp.moveaxis(picked, 2, 0).reshape(slots, -1)
    outgoing_strips = jnp.einsum(
        "dsj,jk->dsk",
        send_select.reshape(devices, CAP, slots),
        strip_values,
        precision=lax.Precision.HIGH,
    )
    outgoing_strips = outgoing_strips + 0.0 * child[0, 0, 0]
    incoming = lax.all_to_all(
        outgoing_strips, ("gx", "gy"), split_axis=0, concat_axis=0, tiled=True
    )
    mine = dest_table == my_index
    rank_all = jnp.cumsum(mine.astype(jnp.int32), axis=1) - 1
    slot_ids = jnp.arange(CAP)
    hits = mine[:, None, :] & (rank_all[:, None, :] == slot_ids[None, :, None])
    chosen = jnp.sum(jnp.where(hits, target_table[:, None, :], 0), axis=2)
    target_rows = jnp.where(jnp.any(hits, axis=2), chosen, -1).reshape(-1)
    row_select = (jnp.arange(crows)[:, None] == target_rows[None, :]).astype(jnp.float32)
    coarse = jnp.einsum(
        "tqs,qsk->tk",
        row_select.reshape(crows, devices, CAP),
        incoming,
        precision=lax.Precision.HIGH,
    )
    counts = jnp.sum(row_select, axis=1)
    boundary = jnp.einsum(
        "tald,de->alte",
        coarse.reshape(crows, 2, levels, STRIP),
        refine_table(STRIP),
        precision=lax.Precision.HIGH,
    )
    divisor = jnp.broadcast_to(1.0 + NUDGE * counts[:, None], (crows, widths))
    factor = 1.0 + child_sppt.astype(jnp.float32)
    edges = (child[:, 0, :], child[:, -1, :], child[:, :, 0].T, child[:, :, -1].T)
    for substep_index in range(SUBSTEPS):
        first_row, last_row, first_col, last_col = edges
        before_x = swap_edge(last_row, "gx", True)
        after_x = swap_edge(first_row, "gx", False)
        before_y = swap_edge(last_col, "gy", True)
        after_y = swap_edge(first_col, "gy", False)
        weight = (substep_index + 1) / 3.0
        child, *edges = substep(
            weight, wind, child, before_x, after_x, before_y, after_y, boundary, factor, divisor
        )
    return (new_parent, child)


def solution(mesh):
    placed = (
        P(None, "gx", "gy"),
        P("gx", "gy"),
        P(None, "gx", "gy"),
        P("gx", "gy"),
        P(),
        P(),
        P(),
        P(),
        P(),
    )

    return jax.shard_map(
        shards,
        mesh=mesh,
        in_specs=placed,
        out_specs=(P(None, "gx", "gy"), P(None, "gx", "gy")),
        check_vma=False,
    )
```

```python
import jax
import jax.numpy as jnp
from jax import lax
from jax.sharding import PartitionSpec as P
from jax.experimental import pallas as pl
from jax.experimental.pallas import tpu as pltpu
import functools

SUBSTEPS = 3
STRIP = 128
CAP = 2


KAPPA = 0.1
VERTICAL = 0.1
NUDGE = 0.5


def edge_halos(block):
    def swap(edge, axis, forward):
        count = lax.axis_size(axis)
        pairs = [(i, i + 1) for i in range(count - 1)]
        if not forward:
            pairs = [(target, source) for source, target in pairs]
        return lax.ppermute(edge, axis, pairs)

    before_x = swap(block[:, -1, :], "gx", True)
    after_x = swap(block[:, 0, :], "gx", False)
    before_y = swap(block[:, :, -1], "gy", True)
    after_y = swap(block[:, :, 0], "gy", False)
    return before_x, after_x, before_y, after_y


def halo_tendency(block, wind_x, wind_y, halos):
    before_x, after_x, before_y, after_y = halos
    north = jnp.concatenate([block[:, 1:, :], after_x[:, None, :]], axis=1)
    south = jnp.concatenate([before_x[:, None, :], block[:, :-1, :]], axis=1)
    east = jnp.concatenate([block[:, :, 1:], after_y[:, :, None]], axis=2)
    west = jnp.concatenate([before_y[:, :, None], block[:, :, :-1]], axis=2)
    laplace = north + south + east + west - 4.0 * block
    return KAPPA * laplace - wind_x * (0.5 * (north - south)) - wind_y * (0.5 * (east - west))


def storm_rows(child, storm_shift, nx, ny):
    levels, crows, widths = child.shape
    devices = nx * ny
    per_level = devices // levels
    piece_rows = crows // per_level
    mine = lax.axis_index(("gx", "gy"))
    pieces = child.reshape(devices, piece_rows, widths)
    gathered = lax.all_to_all(pieces, ("gx", "gy"), 0, 0, tiled=True)
    piece = (mine % per_level) * piece_rows // (crows // storm_shift.shape[1])
    grid = gathered.reshape(nx, ny, piece_rows, widths)
    grid = jnp.roll(grid, storm_shift[0, piece], axis=0)
    grid = jnp.roll(grid, storm_shift[1, piece], axis=1)
    back = lax.all_to_all(grid.reshape(devices, piece_rows, widths), ("gx", "gy"), 0, 0, tiled=True)
    return back.reshape(levels, crows, widths)


def substep_kernel(weight, wind_ref, child_ref, bx_ref, ax_ref, by_ref, ay_ref, bound_ref,
                   factor_ref, divisor_ref, out_ref, first_row_ref, last_row_ref, first_col_ref, last_col_ref):
    levels, rows, cols = child_ref.shape
    row_id = lax.broadcasted_iota(jnp.int32, (rows, cols), 0)
    col_id = lax.broadcasted_iota(jnp.int32, (rows, cols), 1)
    factor = factor_ref[...]
    divisor = divisor_ref[...]
    for l in range(levels):
        c = child_ref[l]
        north = jnp.where(row_id == rows - 1, ax_ref[l:l + 1, :], pltpu.roll(c, rows - 1, 0))
        south = jnp.where(row_id == 0, bx_ref[l:l + 1, :], pltpu.roll(c, 1, 0))
        east = jnp.where(col_id == cols - 1, ay_ref[:, l:l + 1], pltpu.roll(c, cols - 1, 1))
        west = jnp.where(col_id == 0, by_ref[:, l:l + 1], pltpu.roll(c, 1, 1))
        laplace = north + south + east + west - 4.0 * c
        tend = KAPPA * laplace - wind_ref[0, l] * (0.5 * (north - south)) - wind_ref[1, l] * (0.5 * (east - west))
        b0 = bound_ref[0, l]
        target = b0 + weight * (bound_ref[1, l] - b0)
        new = (c + factor * tend + NUDGE * target) / divisor
        out_ref[l] = new
        first_row_ref[l:l + 1, :] = new[0:1, :]
        last_row_ref[l:l + 1, :] = new[rows - 1:rows, :]
        first_col_ref[:, l:l + 1] = new[:, 0:1]
        last_col_ref[:, l:l + 1] = new[:, cols - 1:cols]


def substep(weight, wind, child, bx, ax, by, ay, bound, factor, divisor):
    levels, rows, cols = child.shape
    vmem = pl.BlockSpec(memory_space=pltpu.VMEM)
    smem = pl.BlockSpec(memory_space=pltpu.SMEM)
    f32 = jnp.float32
    return pl.pallas_call(
        functools.partial(substep_kernel, weight),
        out_shape=(
            jax.ShapeDtypeStruct((levels, rows, cols), f32),
            jax.ShapeDtypeStruct((levels, cols), f32),
            jax.ShapeDtypeStruct((levels, cols), f32),
            jax.ShapeDtypeStruct((rows, levels), f32),
            jax.ShapeDtypeStruct((rows, levels), f32),
        ),
        in_specs=[smem] + [vmem] * 8,
        out_specs=(vmem,) * 5,
        cost_estimate=pl.CostEstimate(
            flops=30 * levels * rows * cols, transcendentals=0,
            bytes_accessed=4 * (4 * levels * rows * cols + 2 * rows * cols)),
    )(wind, child, bx, ax, by, ay, bound, factor, divisor)


def swap_edge(edge, axis, forward):
    count = lax.axis_size(axis)
    pairs = [(i, i + 1) for i in range(count - 1)]
    if not forward:
        pairs = [(target, source) for source, target in pairs]
    return lax.ppermute(edge, axis, pairs)


def refine_table(strip):
    coarse = jnp.arange(strip).astype(jnp.float32)
    finer = jnp.arange(3 * strip).astype(jnp.float32)
    position = jnp.clip((finer + 0.5) / 3.0 - 0.5, 0.0, strip - 1.0)
    return jnp.maximum(0.0, 1.0 - jnp.abs(position[None, :] - coarse[:, None]))


def vertical(field):
    upper = jnp.concatenate([field[1:], field[-1:]], axis=0)
    lower = jnp.concatenate([field[:1], field[:-1]], axis=0)
    return upper + lower - 2.0 * field


def shards(
    parent_field,
    parent_sppt,
    child_storm,
    child_sppt,
    wind,
    strip_dest,
    strip_row,
    strip_target,
    storm_shift,
):
    devices = lax.axis_size(("gx", "gy"))
    my_index = lax.axis_index(("gx", "gy"))
    wind_x = wind[0][:, None, None]
    wind_y = wind[1][:, None, None]
    parent_halos = edge_halos(parent_field)
    new_parent = parent_field + (1.0 + parent_sppt.astype(jnp.float32)) * (
        halo_tendency(parent_field, wind_x, wind_y, parent_halos) + VERTICAL * vertical(parent_field)
    )
    levels, crows, widths = child_storm.shape
    nx, ny = lax.axis_size("gx"), lax.axis_size("gy")
    child = storm_rows(child_storm, storm_shift, nx, ny)
    dest_table = strip_dest.reshape(devices, -1)
    row_table = strip_row.reshape(devices, -1)
    target_table = strip_target.reshape(devices, -1)
    slots = dest_table.shape[1]
    my_dest = lax.dynamic_index_in_dim(dest_table, my_index, 0, keepdims=False)
    my_rows = lax.dynamic_index_in_dim(row_table, my_index, 0, keepdims=False)
    same_owner = my_dest[:, None] == my_dest[None, :]
    earlier = jnp.arange(slots)[None, :] < jnp.arange(slots)[:, None]
    rank = jnp.sum((same_owner & earlier).astype(jnp.int32), axis=1)
    slot_index = my_dest * CAP + rank
    send_select = (jnp.arange(devices * CAP)[:, None] == slot_index[None, :]).astype(jnp.float32)
    both_states = jnp.stack([parent_field, new_parent]).reshape(2, levels, -1, STRIP)
    picked = jnp.take(both_states, my_rows, axis=2)
    outgoing_strips = jnp.einsum(
        "dsj,aljk->dsalk",
        send_select.reshape(devices, CAP, slots),
        picked,
        precision=lax.Precision.HIGH,
    )
    outgoing_strips = outgoing_strips + 0.0 * child[0, 0, 0]
    incoming = lax.all_to_all(
        outgoing_strips, ("gx", "gy"), split_axis=0, concat_axis=0, tiled=True
    )
    mine = dest_table == my_index
    rank_all = jnp.cumsum(mine.astype(jnp.int32), axis=1) - 1
    slot_ids = jnp.arange(CAP)
    hits = mine[:, None, :] & (rank_all[:, None, :] == slot_ids[None, :, None])
    chosen = jnp.sum(jnp.where(hits, target_table[:, None, :], 0), axis=2)
    target_rows = jnp.where(jnp.any(hits, axis=2), chosen, -1).reshape(-1)
    row_select = (jnp.arange(crows)[:, None] == target_rows[None, :]).astype(jnp.float32)
    coarse = jnp.einsum(
        "tqs,qsald->altd",
        row_select.reshape(crows, devices, CAP),
        incoming,
        precision=lax.Precision.HIGH,
    )
    counts = jnp.sum(row_select, axis=1)
    boundary = jnp.einsum(
        "altd,de->alte",
        coarse,
        refine_table(STRIP),
        precision=lax.Precision.HIGH,
    )
    divisor = jnp.broadcast_to(1.0 + NUDGE * counts[:, None], (crows, widths))
    factor = 1.0 + child_sppt.astype(jnp.float32)
    edges = (child[:, 0, :], child[:, -1, :], child[:, :, 0].T, child[:, :, -1].T)
    for substep_index in range(SUBSTEPS):
        first_row, last_row, first_col, last_col = edges
        before_x = swap_edge(last_row, "gx", True)
        after_x = swap_edge(first_row, "gx", False)
        before_y = swap_edge(last_col, "gy", True)
        after_y = swap_edge(first_col, "gy", False)
        weight = (substep_index + 1) / 3.0
        child, *edges = substep(
            weight, wind, child, before_x, after_x, before_y, after_y, boundary, factor, divisor
        )
    return (new_parent, child)


def solution(mesh):
    placed = (
        P(None, "gx", "gy"),
        P("gx", "gy"),
        P(None, "gx", "gy"),
        P("gx", "gy"),
        P(),
        P(),
        P(),
        P(),
        P(),
    )

    return jax.shard_map(
        shards,
        mesh=mesh,
        in_specs=placed,
        out_specs=(P(None, "gx", "gy"), P(None, "gx", "gy")),
        check_vma=False,
    )
```

```python
import jax
import jax.numpy as jnp
from jax import lax
from jax.sharding import PartitionSpec as P
from jax.experimental import pallas as pl
from jax.experimental.pallas import tpu as pltpu
import functools

SUBSTEPS = 3
STRIP = 128
CAP = 2


KAPPA = 0.1
VERTICAL = 0.1
NUDGE = 0.5


def edge_halos(block):
    def swap(edge, axis, forward):
        count = lax.axis_size(axis)
        pairs = [(i, i + 1) for i in range(count - 1)]
        if not forward:
            pairs = [(target, source) for source, target in pairs]
        return lax.ppermute(edge, axis, pairs)

    before_x = swap(block[:, -1, :], "gx", True)
    after_x = swap(block[:, 0, :], "gx", False)
    before_y = swap(block[:, :, -1], "gy", True)
    after_y = swap(block[:, :, 0], "gy", False)
    return before_x, after_x, before_y, after_y


def halo_tendency(block, wind_x, wind_y, halos):
    before_x, after_x, before_y, after_y = halos
    north = jnp.concatenate([block[:, 1:, :], after_x[:, None, :]], axis=1)
    south = jnp.concatenate([before_x[:, None, :], block[:, :-1, :]], axis=1)
    east = jnp.concatenate([block[:, :, 1:], after_y[:, :, None]], axis=2)
    west = jnp.concatenate([before_y[:, :, None], block[:, :, :-1]], axis=2)
    laplace = north + south + east + west - 4.0 * block
    return KAPPA * laplace - wind_x * (0.5 * (north - south)) - wind_y * (0.5 * (east - west))


def storm_rows(child, storm_shift, nx, ny):
    levels, crows, widths = child.shape
    devices = nx * ny
    per_level = devices // levels
    piece_rows = crows // per_level
    mine = lax.axis_index(("gx", "gy"))
    pieces = child.reshape(devices, piece_rows, widths)
    gathered = lax.all_to_all(pieces, ("gx", "gy"), 0, 0, tiled=True)
    piece = (mine % per_level) * piece_rows // (crows // storm_shift.shape[1])
    grid = gathered.reshape(nx, ny, piece_rows, widths)
    grid = jnp.roll(grid, storm_shift[0, piece], axis=0)
    grid = jnp.roll(grid, storm_shift[1, piece], axis=1)
    back = lax.all_to_all(grid.reshape(devices, piece_rows, widths), ("gx", "gy"), 0, 0, tiled=True)
    return back.reshape(levels, crows, widths)


def substep_kernel(weight, wind_ref, child_ref, bx_ref, ax_ref, by_ref, ay_ref, bound_ref,
                   factor_ref, divisor_ref, out_ref, first_row_ref, last_row_ref, first_col_ref, last_col_ref):
    levels, rows, cols = child_ref.shape
    row_id = lax.broadcasted_iota(jnp.int32, (rows, cols), 0)
    col_id = lax.broadcasted_iota(jnp.int32, (rows, cols), 1)
    factor = factor_ref[...]
    divisor = divisor_ref[...]
    for l in range(levels):
        c = child_ref[l]
        north = jnp.where(row_id == rows - 1, ax_ref[l:l + 1, :], pltpu.roll(c, rows - 1, 0))
        south = jnp.where(row_id == 0, bx_ref[l:l + 1, :], pltpu.roll(c, 1, 0))
        east = jnp.where(col_id == cols - 1, ay_ref[:, l:l + 1], pltpu.roll(c, cols - 1, 1))
        west = jnp.where(col_id == 0, by_ref[:, l:l + 1], pltpu.roll(c, 1, 1))
        laplace = north + south + east + west - 4.0 * c
        tend = KAPPA * laplace - wind_ref[0, l] * (0.5 * (north - south)) - wind_ref[1, l] * (0.5 * (east - west))
        b0 = bound_ref[0, l]
        target = b0 + weight * (bound_ref[1, l] - b0)
        new = (c + factor * tend + NUDGE * target) / divisor
        out_ref[l] = new
        first_row_ref[l:l + 1, :] = new[0:1, :]
        last_row_ref[l:l + 1, :] = new[rows - 1:rows, :]
        first_col_ref[:, l:l + 1] = new[:, 0:1]
        last_col_ref[:, l:l + 1] = new[:, cols - 1:cols]


def substep(weight, wind, child, bx, ax, by, ay, bound, factor, divisor):
    levels, rows, cols = child.shape
    vmem = pl.BlockSpec(memory_space=pltpu.VMEM)
    smem = pl.BlockSpec(memory_space=pltpu.SMEM)
    f32 = jnp.float32
    return pl.pallas_call(
        functools.partial(substep_kernel, weight),
        out_shape=(
            jax.ShapeDtypeStruct((levels, rows, cols), f32),
            jax.ShapeDtypeStruct((levels, cols), f32),
            jax.ShapeDtypeStruct((levels, cols), f32),
            jax.ShapeDtypeStruct((rows, levels), f32),
            jax.ShapeDtypeStruct((rows, levels), f32),
        ),
        in_specs=[smem] + [vmem] * 8,
        out_specs=(vmem,) * 5,
        cost_estimate=pl.CostEstimate(
            flops=30 * levels * rows * cols, transcendentals=0,
            bytes_accessed=4 * (4 * levels * rows * cols + 2 * rows * cols)),
    )(wind, child, bx, ax, by, ay, bound, factor, divisor)


def swap_edge(edge, axis, forward):
    count = lax.axis_size(axis)
    pairs = [(i, i + 1) for i in range(count - 1)]
    if not forward:
        pairs = [(target, source) for source, target in pairs]
    return lax.ppermute(edge, axis, pairs)


def refine_table(strip):
    coarse = jnp.arange(strip).astype(jnp.float32)
    finer = jnp.arange(3 * strip).astype(jnp.float32)
    position = jnp.clip((finer + 0.5) / 3.0 - 0.5, 0.0, strip - 1.0)
    return jnp.maximum(0.0, 1.0 - jnp.abs(position[None, :] - coarse[:, None]))


def vertical(field):
    upper = jnp.concatenate([field[1:], field[-1:]], axis=0)
    lower = jnp.concatenate([field[:1], field[:-1]], axis=0)
    return upper + lower - 2.0 * field


def shards(
    parent_field,
    parent_sppt,
    child_storm,
    child_sppt,
    wind,
    strip_dest,
    strip_row,
    strip_target,
    storm_shift,
):
    devices = lax.axis_size(("gx", "gy"))
    my_index = lax.axis_index(("gx", "gy"))
    wind_x = wind[0][:, None, None]
    wind_y = wind[1][:, None, None]
    parent_halos = edge_halos(parent_field)
    new_parent = parent_field + (1.0 + parent_sppt.astype(jnp.float32)) * (
        halo_tendency(parent_field, wind_x, wind_y, parent_halos) + VERTICAL * vertical(parent_field)
    )
    levels, crows, widths = child_storm.shape
    nx, ny = lax.axis_size("gx"), lax.axis_size("gy")
    child = storm_rows(child_storm, storm_shift, nx, ny)
    dest_table = strip_dest.reshape(devices, -1)
    row_table = strip_row.reshape(devices, -1)
    target_table = strip_target.reshape(devices, -1)
    slots = dest_table.shape[1]
    my_dest = lax.dynamic_index_in_dim(dest_table, my_index, 0, keepdims=False)
    my_rows = lax.dynamic_index_in_dim(row_table, my_index, 0, keepdims=False)
    same_owner = my_dest[:, None] == my_dest[None, :]
    earlier = jnp.arange(slots)[None, :] < jnp.arange(slots)[:, None]
    rank = jnp.sum((same_owner & earlier).astype(jnp.int32), axis=1)
    slot_index = my_dest * CAP + rank
    send_select = (jnp.arange(devices * CAP)[:, None] == slot_index[None, :]).astype(jnp.float32)
    picked = jnp.stack(
        [jnp.take(state.reshape(levels, -1, STRIP), my_rows, axis=1) for state in (parent_field, new_parent)]
    )
    outgoing_strips = jnp.einsum(
        "dsj,aljk->dsalk",
        send_select.reshape(devices, CAP, slots),
        picked,
        precision=lax.Precision.HIGH,
    )
    outgoing_strips = outgoing_strips + 0.0 * child[0, 0, 0]
    incoming = lax.all_to_all(
        outgoing_strips, ("gx", "gy"), split_axis=0, concat_axis=0, tiled=True
    )
    mine = dest_table == my_index
    rank_all = jnp.cumsum(mine.astype(jnp.int32), axis=1) - 1
    slot_ids = jnp.arange(CAP)
    hits = mine[:, None, :] & (rank_all[:, None, :] == slot_ids[None, :, None])
    chosen = jnp.sum(jnp.where(hits, target_table[:, None, :], 0), axis=2)
    target_rows = jnp.where(jnp.any(hits, axis=2), chosen, -1).reshape(-1)
    row_select = (jnp.arange(crows)[:, None] == target_rows[None, :]).astype(jnp.float32)
    coarse = jnp.einsum(
        "tqs,qsald->altd",
        row_select.reshape(crows, devices, CAP),
        incoming,
        precision=lax.Precision.HIGH,
    )
    counts = jnp.sum(row_select, axis=1)
    boundary = jnp.einsum(
        "altd,de->alte",
        coarse,
        refine_table(STRIP),
        precision=lax.Precision.HIGH,
    )
    divisor = jnp.broadcast_to(1.0 + NUDGE * counts[:, None], (crows, widths))
    factor = 1.0 + child_sppt.astype(jnp.float32)
    edges = (child[:, 0, :], child[:, -1, :], child[:, :, 0].T, child[:, :, -1].T)
    for substep_index in range(SUBSTEPS):
        first_row, last_row, first_col, last_col = edges
        before_x = swap_edge(last_row, "gx", True)
        after_x = swap_edge(first_row, "gx", False)
        before_y = swap_edge(last_col, "gy", True)
        after_y = swap_edge(first_col, "gy", False)
        weight = (substep_index + 1) / 3.0
        child, *edges = substep(
            weight, wind, child, before_x, after_x, before_y, after_y, boundary, factor, divisor
        )
    return (new_parent, child)


def solution(mesh):
    placed = (
        P(None, "gx", "gy"),
        P("gx", "gy"),
        P(None, "gx", "gy"),
        P("gx", "gy"),
        P(),
        P(),
        P(),
        P(),
        P(),
    )

    return jax.shard_map(
        shards,
        mesh=mesh,
        in_specs=placed,
        out_specs=(P(None, "gx", "gy"), P(None, "gx", "gy")),
        check_vma=False,
    )
```
